256 devices in a mesh: node: 16 (over y, x), batch: 16 (over z, core).
Axes of the slice: x: 4, y: 4, z: 8, core: 2. Of those that a mesh axis runs over, the one named last changes fastest.
Arguments:
- inputs: bfloat16 [16, 6, 64, 8192], P('batch', None, None, 'node'), may hold values from -6 to 6
- w_conv: bfloat16 [128, 128], replicated, may hold values from -0.5 to 0.5
- b_conv: float32 [128], replicated, may hold values from -3 to 3
- w_mix: bfloat16 [64, 320], replicated, may hold values from -0.3125 to 0.3125
- b_mix: float32 [64], replicated, may hold values from -3 to 3
- w_skip: bfloat16 [256, 64], replicated, may hold values from -0.75 to 0.75
- b_skip: float32 [256], replicated, may hold values from -3 to 3
- local_fwd: bfloat16 [8192, 384], P('node'), may hold values from -0.25 to 0.25
- local_bwd: bfloat16 [8192, 384], P('node'), may hold values from -0.25 to 0.25
- remote_fwd: bfloat16 [256, 128, 128], P('node'), may hold values from -0.25 to 0.25
- remote_bwd: bfloat16 [256, 128, 128], P('node'), may hold values from -0.25 to 0.25
- tile_src: int32 [256], P('node'), may hold values from 0 to 3, as said below
- tile_dst: int32 [256], P('node'), may hold values from -1 to 3, as said below
- residual_cotangent: bfloat16 [16, 4, 64, 8192], P('batch', None, None, 'node'), may hold values from -6 to 6
- cot_skip: bfloat16 [16, 256, 8192], P('batch', None, 'node'), may hold values from -6 to 6
Outputs:
- residual_out: bfloat16 [16, 4, 64, 8192], P('batch', None, None, 'node')
- skip_out: bfloat16 [16, 256, 8192], P('batch', None, 'node')
- grad_x: bfloat16 [16, 6, 64, 8192], P('batch', None, None, 'node')
- grad_w_conv: float32 [128, 128], replicated
- grad_b_conv: float32 [128], replicated
- grad_w_mix: float32 [64, 320], replicated
- grad_b_mix: float32 [64], replicated
- grad_w_skip: float32 [256, 64], replicated
- grad_b_skip: float32 [256], replicated
The draws below stay inside these ranges and needn't reach their ends.
Inputs may be any that keep to these rules, and one draw needn't show every extreme that they name: `tile_src`: entry p * 16 + q is a block of device p. `tile_dst`: entry p * 16 + q is a block of device q, or -1 where device p holds no tile for device q, always -1 for q = p.
All inputs are finite; a program needn't handle non-finite values.
Results may differ from the reference program's by a relative error of at most 0.012.
Values may be sent and summed in bfloat16 or wider, within the bound.
No kernel may reach another device: no remote copies, remote signals or barrier semaphores. Data moves between devices by JAX's collectives and lax.ppermute only.
A program may use at most 128 MiB of HBM per device.

```python
import math
import jax
import jax.numpy as jnp
from jax import lax

HIDDEN_CHANNELS = 64
SKIP = 256
BLOCK = 128
T_IN = 6
DILATION_GAP = 2
NODE_BLOCKS = 4
OUTPUT_STEPS = 4
NODES = 8192
BATCH = 16
N_NODE = 16


def draw_tile_src(key, part):
    chosen = jax.random.randint(jax.random.fold_in(key, 11), (N_NODE * N_NODE,), 0, NODE_BLOCKS)
    chosen = chosen.at[0].set(0)
    chosen = chosen.at[1].set(NODE_BLOCKS - 1)
    return chosen.astype(jnp.int32)


def draw_tile_dst(key, part):
    levels = jax.random.randint(jax.random.fold_in(key, 13), (N_NODE, 1), 0, 4)
    coin_flip = jax.random.randint(jax.random.fold_in(key, 17), (N_NODE, N_NODE), 0, 4)
    targets = jax.random.randint(jax.random.fold_in(key, 19), (N_NODE, N_NODE), 0, NODE_BLOCKS)
    sender = lax.broadcasted_iota(jnp.int32, (N_NODE, N_NODE), 0)
    receiver = lax.broadcasted_iota(jnp.int32, (N_NODE, N_NODE), 1)
    first_pair = (sender == 0) & (receiver == 1)
    second_pair = (sender == 1) & (receiver == 0)
    live_slot = (coin_flip <= levels) & (sender != receiver) | first_pair | second_pair
    targets = jnp.where(first_pair, NODE_BLOCKS - 1, targets)
    targets = jnp.where(second_pair, 0, targets)
    return jnp.where(live_slot, targets, -1).reshape(N_NODE * N_NODE).astype(jnp.int32)


def level_of(own_key, dims, split, low, high):
    def one(axis_at, shards_of):
        draws = jax.random.uniform(jax.random.fold_in(jax.random.fold_in(own_key, 6), axis_at), (shards_of,), jnp.float32, low / len(split), high / len(split))
        return jnp.repeat(jnp.exp(draws), dims[axis_at] // shards_of).reshape((-1,) + (1,) * (len(dims) - axis_at - 1))

    loudness = one(*split[0])
    for cut in split[1:]:
        loudness = loudness * one(*cut)
    return loudness


def bell_draw(stream_key, shape, scale, reach, split=(), held_as=jnp.bfloat16):
    array = scale * jax.random.normal(stream_key, shape, jnp.float32)
    if split:
        array = array * level_of(stream_key, shape, split, -0.22, 0.18)
    return jnp.clip(array, -reach, reach).astype(held_as)


def setup_inputs(seed: int = 0) -> dict:
    key_of = jax.random.split(jax.random.key(seed), 16)
    inputs = bell_draw(key_of[0], (BATCH, T_IN, HIDDEN_CHANNELS, NODES), 1.0, 6.0, ((0, 16), (3, 16)))
    w_conv = bell_draw(key_of[1], (2 * HIDDEN_CHANNELS, 2 * HIDDEN_CHANNELS), (2 * HIDDEN_CHANNELS) ** -0.5, 0.5)
    b_conv = bell_draw(key_of[2], (2 * HIDDEN_CHANNELS,), 0.5, 3.0, (), jnp.float32)
    w_mix = bell_draw(key_of[3], (HIDDEN_CHANNELS, 5 * HIDDEN_CHANNELS), (5 * HIDDEN_CHANNELS) ** -0.5, 0.3125)
    b_mix = bell_draw(key_of[4], (HIDDEN_CHANNELS,), 0.5, 3.0, (), jnp.float32)
    w_skip = bell_draw(key_of[5], (SKIP, HIDDEN_CHANNELS), HIDDEN_CHANNELS ** -0.5, 0.75)
    b_skip = bell_draw(key_of[6], (SKIP,), 0.5, 3.0, (), jnp.float32)
    local_fwd = bell_draw(key_of[7], (NODES, 3 * BLOCK), (4 * BLOCK) ** -0.5, 0.25, ((0, 16),))
    local_bwd = bell_draw(key_of[8], (NODES, 3 * BLOCK), (4 * BLOCK) ** -0.5, 0.25, ((0, 16),))
    remote_fwd = bell_draw(key_of[9], (N_NODE * N_NODE, BLOCK, BLOCK), (4 * BLOCK) ** -0.5, 0.25, ((0, 16),))
    remote_bwd = bell_draw(key_of[10], (N_NODE * N_NODE, BLOCK, BLOCK), (4 * BLOCK) ** -0.5, 0.25, ((0, 16),))
    tile_src = draw_tile_src(jax.random.fold_in(key_of[15], 71), 0)
    tile_dst = draw_tile_dst(jax.random.fold_in(key_of[15], 71), 0)
    residual_cotangent = bell_draw(key_of[13], (BATCH, OUTPUT_STEPS, HIDDEN_CHANNELS, NODES), 1.0, 6.0, ((0, 16), (3, 16)))
    cot_skip = bell_draw(key_of[14], (BATCH, SKIP, NODES), 1.0, 6.0, ((0, 16), (2, 16)))
    return {"inputs": inputs, "w_conv": w_conv, "b_conv": b_conv, "w_mix": w_mix, "b_mix": b_mix, "w_skip": w_skip, "b_skip": b_skip, "local_fwd": local_fwd, "local_bwd": local_bwd, "remote_fwd": remote_fwd, "remote_bwd": remote_bwd, "tile_src": tile_src, "tile_dst": tile_dst, "residual_cotangent": residual_cotangent, "cot_skip": cot_skip}


def band_forward(values, weights):
    row_count = values.shape[0]
    shaped = values.astype(jnp.float32).reshape(row_count, N_NODE, NODE_BLOCKS, BLOCK)
    zeros_blk = jnp.zeros((row_count, N_NODE, 1, BLOCK), jnp.float32)
    before = jnp.concatenate([zeros_blk, shaped[:, :, :-1]], axis=2)
    after_blk = jnp.concatenate([shaped[:, :, 1:], zeros_blk], axis=2)
    stacked = jnp.concatenate([before, shaped, after_blk], axis=3)
    shaped_w = weights.astype(jnp.float32).reshape(N_NODE, NODE_BLOCKS, BLOCK, 3 * BLOCK)
    result = jnp.einsum('mpik,piak->mpia', stacked, shaped_w)
    return result.reshape(row_count, NODES)

def band_backward(gradient, weights):
    row_count = gradient.shape[0]
    shaped = gradient.astype(jnp.float32).reshape(row_count, N_NODE, NODE_BLOCKS, BLOCK)
    shaped_w = weights.astype(jnp.float32).reshape(N_NODE, NODE_BLOCKS, BLOCK, 3 * BLOCK)
    spread = jnp.einsum('mpia,piak->mpik', shaped, shaped_w).reshape(row_count, N_NODE, NODE_BLOCKS, 3, BLOCK)
    zeros_blk = jnp.zeros((row_count, N_NODE, 1, BLOCK), jnp.float32)
    from_after = jnp.concatenate([spread[:, :, 1:, 0], zeros_blk], axis=2)
    from_before = jnp.concatenate([zeros_blk, spread[:, :, :-1, 2]], axis=2)
    return (spread[:, :, :, 1] + from_after + from_before).reshape(row_count, NODES)

def chooser(indices):
    block_ids = jnp.arange(NODE_BLOCKS, dtype=jnp.int32)
    return (indices.reshape(N_NODE, N_NODE)[:, :, None] == block_ids[None, None, :]).astype(jnp.float32)

def far_forward(values, tile_vals, src_pick, dst_pick):
    row_count = values.shape[0]
    shaped = values.astype(jnp.float32).reshape(row_count, N_NODE, NODE_BLOCKS, BLOCK)
    picked = jnp.einsum('sqi,msic->sqmc', src_pick, shaped)
    product = jnp.einsum('sqmc,sqac->sqma', picked, tile_vals.astype(jnp.float32).reshape(N_NODE, N_NODE, BLOCK, BLOCK))
    product = lax.optimization_barrier(product.astype(jnp.bfloat16)).astype(jnp.float32)
    result = jnp.einsum('sqi,sqma->mqia', dst_pick, product)
    return result.reshape(row_count, NODES)

def far_backward(operands, src_pick, dst_pick):
    summed = None
    for gradient, tile_vals in operands:
        row_count = gradient.shape[0]
        shaped = gradient.astype(jnp.float32).reshape(row_count, N_NODE, NODE_BLOCKS, BLOCK)
        wanted = jnp.einsum('sqi,mqia->sqma', dst_pick, shaped)
        term = jnp.einsum('sqma,sqac->sqmc', wanted, tile_vals.astype(jnp.float32).reshape(N_NODE, N_NODE, BLOCK, BLOCK))
        summed = term if summed is None else summed + term
    summed = lax.optimization_barrier(summed.astype(jnp.bfloat16)).astype(jnp.float32)
    result = jnp.einsum('sqj,sqmc->msjc', src_pick, summed)
    return result.reshape(row_count, NODES)

def reference(inputs, w_conv, b_conv, w_mix, b_mix, w_skip, b_skip, local_fwd, local_bwd, remote_fwd, remote_bwd, tile_src, tile_dst, residual_cotangent, cot_skip):
    src_pick = chooser(tile_src)
    dst_pick = chooser(tile_dst)
    conv_w = w_conv.astype(jnp.float32)
    mix_w = w_mix.astype(jnp.float32)
    skip_w = w_skip.astype(jnp.float32)
    row_count = OUTPUT_STEPS * HIDDEN_CHANNELS

    def diffuse(values, local_w, remote_w):
        return (band_forward(values, local_w) + far_forward(values, remote_w, src_pick, dst_pick)).astype(jnp.bfloat16)

    def window(carried, slices):
        input_window, res_cot, skip_cot = slices
        paired_taps = jnp.concatenate([input_window[:OUTPUT_STEPS], input_window[DILATION_GAP:]], axis=1).astype(jnp.float32)
        pre_act = jnp.einsum('oc,tcn->ton', conv_w, paired_taps) + b_conv[None, :, None]
        filtered = jnp.tanh(pre_act[:, :HIDDEN_CHANNELS])
        gate_val = jax.nn.sigmoid(pre_act[:, HIDDEN_CHANNELS:])
        hidden = (filtered * gate_val).astype(jnp.bfloat16)
        flat_hidden = hidden.reshape(row_count, NODES)
        hop_fwd = diffuse(flat_hidden, local_fwd, remote_fwd)
        hop_bwd = diffuse(flat_hidden, local_bwd, remote_bwd)
        two_fwd = diffuse(hop_fwd, local_fwd, remote_fwd)
        two_bwd = diffuse(hop_bwd, local_bwd, remote_bwd)
        shape3 = (OUTPUT_STEPS, HIDDEN_CHANNELS, NODES)
        parts = jnp.concatenate([hidden, hop_fwd.reshape(shape3), two_fwd.reshape(shape3), hop_bwd.reshape(shape3), two_bwd.reshape(shape3)], axis=1).astype(jnp.float32)
        mixed_features = jnp.einsum('oc,tcn->ton', mix_w, parts) + b_mix[None, :, None]
        residual_stream = (input_window[DILATION_GAP:].astype(jnp.float32) + mixed_features).astype(jnp.bfloat16)
        last_step = hidden[OUTPUT_STEPS - 1].astype(jnp.float32)
        skip_sum = (jnp.dot(skip_w, last_step) + b_skip[:, None]).astype(jnp.bfloat16)
        residual_float32 = res_cot.astype(jnp.float32)
        skip32 = skip_cot.astype(jnp.float32)
        grad_parts = jnp.einsum('co,tcn->ton', mix_w, residual_float32)

        def group(index):
            return grad_parts[:, index * HIDDEN_CHANNELS:(index + 1) * HIDDEN_CHANNELS].reshape(row_count, NODES)
        back2_fwd = group(2).astype(jnp.bfloat16)
        back2_bwd = group(4).astype(jnp.bfloat16)
        back1_fwd = (group(1) + band_backward(back2_fwd, local_fwd) + far_backward([(back2_fwd, remote_fwd)], src_pick, dst_pick)).astype(jnp.bfloat16)
        back1_bwd = (group(3) + band_backward(back2_bwd, local_bwd) + far_backward([(back2_bwd, remote_bwd)], src_pick, dst_pick)).astype(jnp.bfloat16)
        skip_back = jnp.dot(skip_w.T, skip32)
        direct = grad_parts[:, :HIDDEN_CHANNELS].at[OUTPUT_STEPS - 1].add(skip_back).reshape(row_count, NODES)
        summed = direct + band_backward(back1_fwd, local_fwd) + band_backward(back1_bwd, local_bwd)
        summed = summed + far_backward([(back1_fwd, remote_fwd), (back1_bwd, remote_bwd)], src_pick, dst_pick)
        grad_hidden = summed.astype(jnp.bfloat16).reshape(shape3).astype(jnp.float32)
        grad_pre = jnp.concatenate([grad_hidden * gate_val * (1.0 - filtered * filtered), grad_hidden * filtered * gate_val * (1.0 - gate_val)], axis=1).astype(jnp.bfloat16).astype(jnp.float32)
        tap_gradients = jnp.einsum('oc,ton->tcn', conv_w, grad_pre)
        input_gradient = jnp.zeros((T_IN, HIDDEN_CHANNELS, NODES), jnp.float32)
        input_gradient = input_gradient.at[:OUTPUT_STEPS].add(tap_gradients[:, :HIDDEN_CHANNELS])
        input_gradient = input_gradient.at[DILATION_GAP:].add(tap_gradients[:, HIDDEN_CHANNELS:] + residual_float32)
        updates = (jnp.einsum('ton,tcn->oc', grad_pre, paired_taps), lax.optimization_barrier(jnp.sum(grad_pre, axis=(0, 2))), jnp.einsum('tcn,ton->co', residual_float32, parts), lax.optimization_barrier(jnp.sum(residual_float32, axis=(0, 2))), jnp.dot(skip32, last_step.T), lax.optimization_barrier(jnp.sum(skip32, axis=1)))
        carried = tuple((old + new for old, new in zip(carried, updates)))
        return (carried, (residual_stream, skip_sum, input_gradient.astype(jnp.bfloat16)))
    start = (jnp.zeros((2 * HIDDEN_CHANNELS, 2 * HIDDEN_CHANNELS), jnp.float32), jnp.zeros((2 * HIDDEN_CHANNELS,), jnp.float32), jnp.zeros((HIDDEN_CHANNELS, 5 * HIDDEN_CHANNELS), jnp.float32), jnp.zeros((HIDDEN_CHANNELS,), jnp.float32), jnp.zeros((SKIP, HIDDEN_CHANNELS), jnp.float32), jnp.zeros((SKIP,), jnp.float32))
    totals, outputs = lax.scan(window, start, (inputs, residual_cotangent, cot_skip))
    grad_scale = 1.0 / math.sqrt(float(BATCH * NODES * OUTPUT_STEPS))
    return (outputs[0], outputs[1], outputs[2], totals[0] * grad_scale, totals[1] * grad_scale, totals[2] * grad_scale, totals[3] * grad_scale, totals[4] * grad_scale, totals[5] * grad_scale)
```

```python
import math

import jax
import jax.numpy as jnp
from jax import lax
from jax.sharding import PartitionSpec as P

DILATION_GAP = 2


def neighbor_stack(values, blocks, tile_width):
    row_count = values.shape[0]
    shaped = values.reshape(row_count, blocks, tile_width)
    zeros_blk = jnp.zeros((row_count, 1, tile_width), values.dtype)
    before = jnp.concatenate([zeros_blk, shaped[:, :-1]], axis=1)
    after_blk = jnp.concatenate([shaped[:, 1:], zeros_blk], axis=1)
    return jnp.concatenate([before, shaped, after_blk], axis=2)


def band_apply(values, weights):
    tile_width = weights.shape[1] // 3
    blocks = weights.shape[0] // tile_width
    stacked = neighbor_stack(values, blocks, tile_width)
    shaped_w = weights.reshape(blocks, tile_width, 3 * tile_width)
    result = jnp.einsum("mik,iak->mia", stacked, shaped_w, preferred_element_type=jnp.float32)
    return result.reshape(values.shape[0], blocks * tile_width)


def band_transpose(gradient, weights):
    tile_width = weights.shape[1] // 3
    blocks = weights.shape[0] // tile_width
    row_count = gradient.shape[0]
    shaped_w = weights.reshape(blocks, tile_width, 3 * tile_width)
    spread = jnp.einsum(
        "mia,iak->mik",
        gradient.reshape(row_count, blocks, tile_width),
        shaped_w,
        preferred_element_type=jnp.float32,
    )
    spread = spread.reshape(row_count, blocks, 3, tile_width)
    zeros_blk = jnp.zeros((row_count, 1, tile_width), jnp.float32)
    from_after = jnp.concatenate([spread[:, 1:, 0], zeros_blk], axis=1)
    from_before = jnp.concatenate([zeros_blk, spread[:, :-1, 2]], axis=1)
    return (spread[:, :, 1] + from_after + from_before).reshape(row_count, blocks * tile_width)


def pick_blocks(values, chooser):
    blocks = chooser.shape[1]
    shaped = values.reshape(values.shape[0], blocks, values.shape[1] // blocks)
    return jnp.einsum("qi,mic->qmc", chooser, shaped, preferred_element_type=jnp.float32).astype(
        jnp.bfloat16
    )


def place_blocks(pieces, chooser):
    result = jnp.einsum("qi,qmc->mic", chooser, pieces, preferred_element_type=jnp.float32)
    return result.reshape(result.shape[0], result.shape[1] * result.shape[2])


def tile_forward(pieces, tile_vals):
    return jnp.einsum("qmc,qac->qma", pieces, tile_vals, preferred_element_type=jnp.float32).astype(
        jnp.bfloat16
    )


def tile_backward(pieces, tile_vals):
    return jnp.einsum("qma,qac->qmc", pieces, tile_vals, preferred_element_type=jnp.float32)


def exchange_sum(pieces):
    sizes = [piece.size for piece in pieces]
    flat = jnp.concatenate([piece.reshape(-1) for piece in pieces])
    node_count = lax.axis_size("node")
    batch_count = lax.axis_size("batch")
    group = node_count * batch_count
    total = flat.shape[0]
    padded = -(-total // group) * group
    flat = jnp.pad(flat, (0, padded - total))
    part = lax.all_to_all(
        flat.reshape(node_count, padded // node_count), "node", 0, 0, tiled=True
    ).sum(axis=0)
    part = lax.all_to_all(
        part.reshape(batch_count, padded // group), "batch", 0, 0, tiled=True
    ).sum(axis=0)
    spread = jnp.broadcast_to(part[None], (batch_count, padded // group))
    spread = lax.all_to_all(spread, "batch", 0, 0, tiled=True).reshape(padded // node_count)
    spread = jnp.broadcast_to(spread[None], (node_count, padded // node_count))
    spread = lax.all_to_all(spread, "node", 0, 0, tiled=True).reshape(padded)
    results = []
    offset = 0
    for piece, size in zip(pieces, sizes):
        results.append(spread[offset : offset + size].reshape(piece.shape))
        offset += size
    return tuple(results)


def shards(
    inputs,
    w_conv,
    b_conv,
    w_mix,
    b_mix,
    w_skip,
    b_skip,
    local_fwd,
    local_bwd,
    remote_fwd,
    remote_bwd,
    tile_src,
    tile_dst,
    residual_cotangent,
    cot_skip,
):
    windows, input_steps, channel_count, local_nodes = inputs.shape
    output_steps = input_steps - DILATION_GAP
    tile_width = remote_fwd.shape[1]
    blocks = local_nodes // tile_width
    block_ids = jnp.arange(blocks, dtype=jnp.int32)
    own_src = (tile_src[:, None] == block_ids[None, :]).astype(jnp.bfloat16)
    own_dst = (tile_dst[:, None] == block_ids[None, :]).astype(jnp.bfloat16)
    row_count = windows * output_steps * channel_count
    shape4 = (windows, output_steps, channel_count, local_nodes)
    paired_taps = jnp.concatenate([inputs[:, :output_steps], inputs[:, DILATION_GAP:]], axis=2)
    pre_act = (
        jnp.einsum("oc,wtcn->wton", w_conv, paired_taps, preferred_element_type=jnp.float32)
        + b_conv[None, None, :, None]
    )
    filtered = jnp.tanh(pre_act[:, :, :channel_count])
    gate_val = jax.nn.sigmoid(pre_act[:, :, channel_count:])
    hidden = (filtered * gate_val).astype(jnp.bfloat16)
    flat_hidden = hidden.reshape(row_count, local_nodes)

    def push_hop(picked_fwd, picked_bwd):
        part_fwd = tile_forward(picked_fwd, remote_fwd)
        part_bwd = tile_forward(picked_bwd, remote_bwd)
        got_fwd, got_bwd, got_dst = (
            lax.all_to_all(part_fwd, "node", split_axis=0, concat_axis=0, tiled=True),
            lax.all_to_all(part_bwd, "node", split_axis=0, concat_axis=0, tiled=True),
            lax.all_to_all(own_dst, "node", split_axis=0, concat_axis=0, tiled=True),
        )
        return (place_blocks(got_fwd, got_dst), place_blocks(got_bwd, got_dst), got_dst)

    picked = pick_blocks(flat_hidden, own_src)
    far_fwd, far_bwd, recv_dst = push_hop(picked, picked)
    hop_fwd = (band_apply(flat_hidden, local_fwd) + far_fwd).astype(jnp.bfloat16)
    hop_bwd = (band_apply(flat_hidden, local_bwd) + far_bwd).astype(jnp.bfloat16)
    far_fwd, far_bwd, recv_dst = push_hop(
        pick_blocks(hop_fwd, own_src), pick_blocks(hop_bwd, own_src)
    )
    two_fwd = (band_apply(hop_fwd, local_fwd) + far_fwd).astype(jnp.bfloat16)
    two_bwd = (band_apply(hop_bwd, local_bwd) + far_bwd).astype(jnp.bfloat16)
    stacked_parts = jnp.concatenate(
        [
            hidden,
            hop_fwd.reshape(shape4),
            two_fwd.reshape(shape4),
            hop_bwd.reshape(shape4),
            two_bwd.reshape(shape4),
        ],
        axis=2,
    )
    mixed_features = (
        jnp.einsum("oc,wtcn->wton", w_mix, stacked_parts, preferred_element_type=jnp.float32)
        + b_mix[None, None, :, None]
    )
    residual_stream = (inputs[:, DILATION_GAP:].astype(jnp.float32) + mixed_features).astype(
        jnp.bfloat16
    )
    last_step = hidden[:, output_steps - 1]
    skip_sum = (
        jnp.einsum("sc,wcn->wsn", w_skip, last_step, preferred_element_type=jnp.float32)
        + b_skip[None, :, None]
    ).astype(jnp.bfloat16)
    grad_parts = jnp.einsum(
        "co,wtcn->wton", w_mix, residual_cotangent, preferred_element_type=jnp.float32
    )
    grad_mix = jnp.einsum(
        "wtcn,wton->co", residual_cotangent, stacked_parts, preferred_element_type=jnp.float32
    )
    grad_bmix = jnp.sum(residual_cotangent.astype(jnp.float32), axis=(0, 1, 3))
    grad_skip = jnp.einsum("wsn,wcn->sc", cot_skip, last_step, preferred_element_type=jnp.float32)
    grad_bskip = jnp.sum(cot_skip.astype(jnp.float32), axis=(0, 2))

    def group_of(index):
        return grad_parts[:, :, index * channel_count : (index + 1) * channel_count].reshape(
            row_count, local_nodes
        )

    back2_fwd = group_of(2).astype(jnp.bfloat16)
    back2_bwd = group_of(4).astype(jnp.bfloat16)

    def fetch_rows(grad_fwd, grad_bwd):
        return (
            lax.all_to_all(
                pick_blocks(grad_fwd, recv_dst), "node", split_axis=0, concat_axis=0, tiled=True
            ),
            lax.all_to_all(
                pick_blocks(grad_bwd, recv_dst), "node", split_axis=0, concat_axis=0, tiled=True
            ),
        )

    got_fwd, got_bwd = fetch_rows(back2_fwd, back2_bwd)
    near1_fwd = place_blocks(tile_backward(got_fwd, remote_fwd).astype(jnp.bfloat16), own_src)
    near1_bwd = place_blocks(tile_backward(got_bwd, remote_bwd).astype(jnp.bfloat16), own_src)
    back1_fwd = (group_of(1) + band_transpose(back2_fwd, local_fwd) + near1_fwd).astype(
        jnp.bfloat16
    )
    back1_bwd = (group_of(3) + band_transpose(back2_bwd, local_bwd) + near1_bwd).astype(
        jnp.bfloat16
    )
    got_fwd, got_bwd = fetch_rows(back1_fwd, back1_bwd)
    combined = (tile_backward(got_fwd, remote_fwd) + tile_backward(got_bwd, remote_bwd)).astype(
        jnp.bfloat16
    )
    far_total = place_blocks(combined, own_src)
    skip_back = jnp.einsum("sc,wsn->wcn", w_skip, cot_skip, preferred_element_type=jnp.float32)
    direct = (
        grad_parts[:, :, :channel_count]
        .at[:, output_steps - 1]
        .add(skip_back)
        .reshape(row_count, local_nodes)
    )
    summed = (
        direct
        + band_transpose(back1_fwd, local_fwd)
        + band_transpose(back1_bwd, local_bwd)
        + far_total
    )
    grad_hidden = summed.astype(jnp.bfloat16).reshape(shape4).astype(jnp.float32)
    grad_pre = jnp.concatenate(
        [
            grad_hidden * gate_val * (1.0 - filtered * filtered),
            grad_hidden * filtered * gate_val * (1.0 - gate_val),
        ],
        axis=2,
    ).astype(jnp.bfloat16)
    tap_gradients = jnp.einsum(
        "oc,wton->wtcn", w_conv, grad_pre, preferred_element_type=jnp.float32
    )
    input_gradient = jnp.zeros((windows, input_steps, channel_count, local_nodes), jnp.float32)
    input_gradient = input_gradient.at[:, :output_steps].add(tap_gradients[:, :, :channel_count])
    input_gradient = input_gradient.at[:, DILATION_GAP:].add(
        tap_gradients[:, :, channel_count:] + residual_cotangent.astype(jnp.float32)
    )
    grad_wconv = jnp.einsum(
        "wton,wtcn->oc", grad_pre, paired_taps, preferred_element_type=jnp.float32
    )
    grad_bconv = jnp.sum(grad_pre.astype(jnp.float32), axis=(0, 1, 3))
    totals = exchange_sum((grad_wconv, grad_bconv, grad_mix, grad_bmix, grad_skip, grad_bskip))
    grad_count = (
        windows * lax.axis_size("batch") * local_nodes * lax.axis_size("node") * output_steps
    )
    grad_scale = 1.0 / math.sqrt(float(grad_count))
    return (
        residual_stream,
        skip_sum,
        input_gradient.astype(jnp.bfloat16),
        totals[0] * grad_scale,
        totals[1] * grad_scale,
        totals[2] * grad_scale,
        totals[3] * grad_scale,
        totals[4] * grad_scale,
        totals[5] * grad_scale,
    )


def solution(mesh):
    return jax.shard_map(
        shards,
        mesh=mesh,
        in_specs=(
            P("batch", None, None, "node"),
            P(),
            P(),
            P(),
            P(),
            P(),
            P(),
            P("node", None),
            P("node", None),
            P("node", None, None),
            P("node", None, None),
            P("node"),
            P("node"),
            P("batch", None, None, "node"),
            P("batch", None, "node"),
        ),
        out_specs=(
            P("batch", None, None, "node"),
            P("batch", None, "node"),
            P("batch", None, None, "node"),
            P(),
            P(),
            P(),
            P(),
            P(),
            P(),
        ),
        check_vma=False,
    )
```

```python
import math

import jax
import jax.numpy as jnp
from jax import lax
from jax.sharding import PartitionSpec as P

DILATION_GAP = 2


def neighbor_stack(values, blocks, tile_width):
    row_count = values.shape[0]
    shaped = values.reshape(row_count, blocks, tile_width)
    zeros_blk = jnp.zeros((row_count, 1, tile_width), values.dtype)
    before = jnp.concatenate([zeros_blk, shaped[:, :-1]], axis=1)
    after_blk = jnp.concatenate([shaped[:, 1:], zeros_blk], axis=1)
    return jnp.concatenate([before, shaped, after_blk], axis=2)


def band_apply(values, weights):
    tile_width = weights.shape[1] // 3
    blocks = weights.shape[0] // tile_width
    stacked = neighbor_stack(values, blocks, tile_width)
    shaped_w = weights.reshape(blocks, tile_width, 3 * tile_width)
    result = jnp.einsum("mik,iak->mia", stacked, shaped_w, preferred_element_type=jnp.float32)
    return result.reshape(values.shape[0], blocks * tile_width)


def band_transpose(gradient, weights):
    tile_width = weights.shape[1] // 3
    blocks = weights.shape[0] // tile_width
    row_count = gradient.shape[0]
    shaped_w = weights.reshape(blocks, tile_width, 3 * tile_width)
    spread = jnp.einsum(
        "mia,iak->mik",
        gradient.reshape(row_count, blocks, tile_width),
        shaped_w,
        preferred_element_type=jnp.float32,
    )
    spread = spread.reshape(row_count, blocks, 3, tile_width)
    zeros_blk = jnp.zeros((row_count, 1, tile_width), jnp.float32)
    from_after = jnp.concatenate([spread[:, 1:, 0], zeros_blk], axis=1)
    from_before = jnp.concatenate([zeros_blk, spread[:, :-1, 2]], axis=1)
    return (spread[:, :, 1] + from_after + from_before).reshape(row_count, blocks * tile_width)


def pick_blocks(values, chooser):
    blocks = chooser.shape[1]
    shaped = values.reshape(values.shape[0], blocks, values.shape[1] // blocks)
    return jnp.einsum("qi,mic->qmc", chooser, shaped, preferred_element_type=jnp.float32).astype(
        jnp.bfloat16
    )


def place_blocks(pieces, chooser):
    result = jnp.einsum("qi,qmc->mic", chooser, pieces, preferred_element_type=jnp.float32)
    return result.reshape(result.shape[0], result.shape[1] * result.shape[2])


def tile_forward(pieces, tile_vals):
    return jnp.einsum("qmc,qac->qma", pieces, tile_vals, preferred_element_type=jnp.float32).astype(
        jnp.bfloat16
    )


def tile_backward(pieces, tile_vals):
    return jnp.einsum("qma,qac->qmc", pieces, tile_vals, preferred_element_type=jnp.float32)


def exchange_sum(pieces):
    sizes = [piece.size for piece in pieces]
    flat = jnp.concatenate([piece.reshape(-1) for piece in pieces])
    node_count = lax.axis_size("node")
    batch_count = lax.axis_size("batch")
    total = flat.shape[0]
    padded = -(-total // node_count) * node_count
    flat = jnp.pad(flat, (0, padded - total))
    part = lax.all_to_all(
        flat.reshape(node_count, padded // node_count), "node", 0, 0, tiled=True
    ).sum(axis=0)
    part = jnp.broadcast_to(part[None], (batch_count, padded // node_count))
    part = lax.all_to_all(part, "batch", 0, 0, tiled=True).sum(axis=0)
    spread = jnp.broadcast_to(part[None], (node_count, padded // node_count))
    spread = lax.all_to_all(spread, "node", 0, 0, tiled=True).reshape(padded)
    results = []
    offset = 0
    for piece, size in zip(pieces, sizes):
        results.append(spread[offset : offset + size].reshape(piece.shape))
        offset += size
    return tuple(results)


def shards(
    inputs,
    w_conv,
    b_conv,
    w_mix,
    b_mix,
    w_skip,
    b_skip,
    local_fwd,
    local_bwd,
    remote_fwd,
    remote_bwd,
    tile_src,
    tile_dst,
    residual_cotangent,
    cot_skip,
):
    windows, input_steps, channel_count, local_nodes = inputs.shape
    output_steps = input_steps - DILATION_GAP
    tile_width = remote_fwd.shape[1]
    blocks = local_nodes // tile_width
    block_ids = jnp.arange(blocks, dtype=jnp.int32)
    own_src = (tile_src[:, None] == block_ids[None, :]).astype(jnp.bfloat16)
    own_dst = (tile_dst[:, None] == block_ids[None, :]).astype(jnp.bfloat16)
    row_count = windows * output_steps * channel_count
    shape4 = (windows, output_steps, channel_count, local_nodes)
    paired_taps = jnp.concatenate([inputs[:, :output_steps], inputs[:, DILATION_GAP:]], axis=2)
    pre_act = (
        jnp.einsum("oc,wtcn->wton", w_conv, paired_taps, preferred_element_type=jnp.float32)
        + b_conv[None, None, :, None]
    )
    filtered = jnp.tanh(pre_act[:, :, :channel_count])
    gate_val = jax.nn.sigmoid(pre_act[:, :, channel_count:])
    hidden = (filtered * gate_val).astype(jnp.bfloat16)
    flat_hidden = hidden.reshape(row_count, local_nodes)

    def push_hop(picked_fwd, picked_bwd):
        part_fwd = tile_forward(picked_fwd, remote_fwd)
        part_bwd = tile_forward(picked_bwd, remote_bwd)
        got_both = lax.all_to_all(
            jnp.concatenate([part_fwd, part_bwd], axis=1),
            "node",
            split_axis=0,
            concat_axis=0,
            tiled=True,
        )
        got_fwd, got_bwd = got_both[:, :row_count], got_both[:, row_count:]
        got_dst = lax.all_to_all(own_dst, "node", split_axis=0, concat_axis=0, tiled=True)
        return (place_blocks(got_fwd, got_dst), place_blocks(got_bwd, got_dst), got_dst)

    picked = pick_blocks(flat_hidden, own_src)
    far_fwd, far_bwd, recv_dst = push_hop(picked, picked)
    hop_fwd = (band_apply(flat_hidden, local_fwd) + far_fwd).astype(jnp.bfloat16)
    hop_bwd = (band_apply(flat_hidden, local_bwd) + far_bwd).astype(jnp.bfloat16)
    far_fwd, far_bwd, recv_dst = push_hop(
        pick_blocks(hop_fwd, own_src), pick_blocks(hop_bwd, own_src)
    )
    two_fwd = (band_apply(hop_fwd, local_fwd) + far_fwd).astype(jnp.bfloat16)
    two_bwd = (band_apply(hop_bwd, local_bwd) + far_bwd).astype(jnp.bfloat16)
    stacked_parts = jnp.concatenate(
        [
            hidden,
            hop_fwd.reshape(shape4),
            two_fwd.reshape(shape4),
            hop_bwd.reshape(shape4),
            two_bwd.reshape(shape4),
        ],
        axis=2,
    )
    mixed_features = (
        jnp.einsum("oc,wtcn->wton", w_mix, stacked_parts, preferred_element_type=jnp.float32)
        + b_mix[None, None, :, None]
    )
    residual_stream = (inputs[:, DILATION_GAP:].astype(jnp.float32) + mixed_features).astype(
        jnp.bfloat16
    )
    last_step = hidden[:, output_steps - 1]
    skip_sum = (
        jnp.einsum("sc,wcn->wsn", w_skip, last_step, preferred_element_type=jnp.float32)
        + b_skip[None, :, None]
    ).astype(jnp.bfloat16)
    grad_parts = jnp.einsum(
        "co,wtcn->wton", w_mix, residual_cotangent, preferred_element_type=jnp.float32
    )
    grad_mix = jnp.einsum(
        "wtcn,wton->co", residual_cotangent, stacked_parts, preferred_element_type=jnp.float32
    )
    grad_bmix = jnp.sum(residual_cotangent.astype(jnp.float32), axis=(0, 1, 3))
    grad_skip = jnp.einsum("wsn,wcn->sc", cot_skip, last_step, preferred_element_type=jnp.float32)
    grad_bskip = jnp.sum(cot_skip.astype(jnp.float32), axis=(0, 2))

    def group_of(index):
        return grad_parts[:, :, index * channel_count : (index + 1) * channel_count].reshape(
            row_count, local_nodes
        )

    back2_fwd = group_of(2).astype(jnp.bfloat16)
    back2_bwd = group_of(4).astype(jnp.bfloat16)

    def fetch_rows(grad_fwd, grad_bwd):
        got_both = lax.all_to_all(
            jnp.concatenate(
                [pick_blocks(grad_fwd, recv_dst), pick_blocks(grad_bwd, recv_dst)], axis=1
            ),
            "node",
            split_axis=0,
            concat_axis=0,
            tiled=True,
        )
        return got_both[:, :row_count], got_both[:, row_count:]

    got_fwd, got_bwd = fetch_rows(back2_fwd, back2_bwd)
    near1_fwd = place_blocks(tile_backward(got_fwd, remote_fwd).astype(jnp.bfloat16), own_src)
    near1_bwd = place_blocks(tile_backward(got_bwd, remote_bwd).astype(jnp.bfloat16), own_src)
    back1_fwd = (group_of(1) + band_transpose(back2_fwd, local_fwd) + near1_fwd).astype(
        jnp.bfloat16
    )
    back1_bwd = (group_of(3) + band_transpose(back2_bwd, local_bwd) + near1_bwd).astype(
        jnp.bfloat16
    )
    got_fwd, got_bwd = fetch_rows(back1_fwd, back1_bwd)
    combined = (tile_backward(got_fwd, remote_fwd) + tile_backward(got_bwd, remote_bwd)).astype(
        jnp.bfloat16
    )
    far_total = place_blocks(combined, own_src)
    skip_back = jnp.einsum("sc,wsn->wcn", w_skip, cot_skip, preferred_element_type=jnp.float32)
    direct = (
        grad_parts[:, :, :channel_count]
        .at[:, output_steps - 1]
        .add(skip_back)
        .reshape(row_count, local_nodes)
    )
    summed = (
        direct
        + band_transpose(back1_fwd, local_fwd)
        + band_transpose(back1_bwd, local_bwd)
        + far_total
    )
    grad_hidden = summed.astype(jnp.bfloat16).reshape(shape4).astype(jnp.float32)
    grad_pre = jnp.concatenate(
        [
            grad_hidden * gate_val * (1.0 - filtered * filtered),
            grad_hidden * filtered * gate_val * (1.0 - gate_val),
        ],
        axis=2,
    ).astype(jnp.bfloat16)
    tap_gradients = jnp.einsum(
        "oc,wton->wtcn", w_conv, grad_pre, preferred_element_type=jnp.float32
    )
    input_gradient = jnp.zeros((windows, input_steps, channel_count, local_nodes), jnp.float32)
    input_gradient = input_gradient.at[:, :output_steps].add(tap_gradients[:, :, :channel_count])
    input_gradient = input_gradient.at[:, DILATION_GAP:].add(
        tap_gradients[:, :, channel_count:] + residual_cotangent.astype(jnp.float32)
    )
    grad_wconv = jnp.einsum(
        "wton,wtcn->oc", grad_pre, paired_taps, preferred_element_type=jnp.float32
    )
    grad_bconv = jnp.sum(grad_pre.astype(jnp.float32), axis=(0, 1, 3))
    totals = exchange_sum((grad_wconv, grad_bconv, grad_mix, grad_bmix, grad_skip, grad_bskip))
    grad_count = (
        windows * lax.axis_size("batch") * local_nodes * lax.axis_size("node") * output_steps
    )
    grad_scale = 1.0 / math.sqrt(float(grad_count))
    return (
        residual_stream,
        skip_sum,
        input_gradient.astype(jnp.bfloat16),
        totals[0] * grad_scale,
        totals[1] * grad_scale,
        totals[2] * grad_scale,
        totals[3] * grad_scale,
        totals[4] * grad_scale,
        totals[5] * grad_scale,
    )


def solution(mesh):
    return jax.shard_map(
        shards,
        mesh=mesh,
        in_specs=(
            P("batch", None, None, "node"),
            P(),
            P(),
            P(),
            P(),
            P(),
            P(),
            P("node", None),
            P("node", None),
            P("node", None, None),
            P("node", None, None),
            P("node"),
            P("node"),
            P("batch", None, None, "node"),
            P("batch", None, "node"),
        ),
        out_specs=(
            P("batch", None, None, "node"),
            P("batch", None, "node"),
            P("batch", None, None, "node"),
            P(),
            P(),
            P(),
            P(),
            P(),
            P(),
        ),
        check_vma=False,
    )
```

```python
import math

import jax
import jax.numpy as jnp
from jax import lax
from jax.sharding import PartitionSpec as P

DILATION_GAP = 2


def dense_band(weights, blocks, tile_width):
    shaped = weights.reshape(blocks, tile_width, 1, 3, tile_width)
    row_ids = lax.broadcasted_iota(jnp.int32, (blocks, 1, blocks, 3, 1), 0)
    col_ids = lax.broadcasted_iota(jnp.int32, (blocks, 1, blocks, 3, 1), 2)
    offsets = lax.broadcasted_iota(jnp.int32, (blocks, 1, blocks, 3, 1), 3)
    hits = (col_ids == row_ids + offsets - 1).astype(weights.dtype)
    placed = (shaped * hits).sum(axis=3, dtype=jnp.float32).astype(weights.dtype)
    return placed.reshape(blocks * tile_width, blocks * tile_width)


def spread_onehot(chooser, tile_vals):
    slots, blocks = chooser.shape
    tile_width = tile_vals.shape[2]
    placed = tile_vals[:, :, None, :] * chooser[:, None, :, None]
    return placed.reshape(slots, tile_vals.shape[1], blocks * tile_width)


def near_apply(values, dense):
    return jnp.einsum("mn,kn->mk", values, dense, preferred_element_type=jnp.float32)


def near_transpose(gradient, dense):
    return jnp.einsum("mk,kn->mn", gradient, dense, preferred_element_type=jnp.float32)


def tile_products(values, spread_tiles):
    return jnp.einsum(
        "mn,qan->qma", values, spread_tiles, preferred_element_type=jnp.float32
    ).astype(jnp.bfloat16)


def place_rows(pieces, placer):
    return jnp.einsum("sma,san->mn", pieces, placer, preferred_element_type=jnp.float32)


def pick_rows(values, placer):
    return jnp.einsum(
        "mn,san->sma", values, placer, preferred_element_type=jnp.float32
    ).astype(jnp.bfloat16)


def tile_backward(pieces, tile_vals):
    return jnp.einsum("qma,qac->qmc", pieces, tile_vals, preferred_element_type=jnp.float32)


def exchange_sum(pieces):
    sizes = [piece.size for piece in pieces]
    flat = jnp.concatenate([piece.reshape(-1) for piece in pieces])
    node_count = lax.axis_size("node")
    batch_count = lax.axis_size("batch")
    total = flat.shape[0]
    padded = -(-total // node_count) * node_count
    flat = jnp.pad(flat, (0, padded - total))
    part = lax.all_to_all(
        flat.reshape(node_count, padded // node_count), "node", 0, 0, tiled=True
    ).sum(axis=0)
    part = jnp.broadcast_to(part[None], (batch_count, padded // node_count))
    part = lax.all_to_all(part, "batch", 0, 0, tiled=True).sum(axis=0)
    spread = jnp.broadcast_to(part[None], (node_count, padded // node_count))
    spread = lax.all_to_all(spread, "node", 0, 0, tiled=True).reshape(padded)
    results = []
    offset = 0
    for piece, size in zip(pieces, sizes):
        results.append(spread[offset : offset + size].reshape(piece.shape))
        offset += size
    return tuple(results)


def shards(
    inputs,
    w_conv,
    b_conv,
    w_mix,
    b_mix,
    w_skip,
    b_skip,
    local_fwd,
    local_bwd,
    remote_fwd,
    remote_bwd,
    tile_src,
    tile_dst,
    residual_cotangent,
    cot_skip,
):
    windows, input_steps, channel_count, local_nodes = inputs.shape
    output_steps = input_steps - DILATION_GAP
    tile_width = remote_fwd.shape[1]
    blocks = local_nodes // tile_width
    block_ids = jnp.arange(blocks, dtype=jnp.int32)
    own_src = (tile_src[:, None] == block_ids[None, :]).astype(jnp.bfloat16)
    own_dst = (tile_dst[:, None] == block_ids[None, :]).astype(jnp.bfloat16)
    row_count = windows * output_steps * channel_count
    shape4 = (windows, output_steps, channel_count, local_nodes)
    paired_taps = jnp.concatenate([inputs[:, :output_steps], inputs[:, DILATION_GAP:]], axis=2)
    pre_act = (
        jnp.einsum("oc,wtcn->wton", w_conv, paired_taps, preferred_element_type=jnp.float32)
        + b_conv[None, None, :, None]
    )
    filtered = jnp.tanh(pre_act[:, :, :channel_count])
    gate_val = jax.nn.sigmoid(pre_act[:, :, channel_count:])
    hidden = (filtered * gate_val).astype(jnp.bfloat16)
    flat_hidden = hidden.reshape(row_count, local_nodes)
    eye_tile = jnp.eye(tile_width, dtype=jnp.bfloat16)
    eye_slots = jnp.broadcast_to(eye_tile, (own_src.shape[0], tile_width, tile_width))
    dense_fwd = dense_band(local_fwd, blocks, tile_width)
    dense_bwd = dense_band(local_bwd, blocks, tile_width)
    spread_fwd = spread_onehot(own_src, remote_fwd)
    spread_bwd = spread_onehot(own_src, remote_bwd)
    src_placer = spread_onehot(own_src, eye_slots)
    recv_dst = lax.all_to_all(own_dst, "node", split_axis=0, concat_axis=0, tiled=True)
    dst_placer = spread_onehot(recv_dst, eye_slots)

    def swap(first, second):
        got_both = lax.all_to_all(
            jnp.concatenate([first, second], axis=1),
            "node",
            split_axis=0,
            concat_axis=0,
            tiled=True,
        )
        return got_both[:, :row_count], got_both[:, row_count:]

    def push_hop(values_fwd, values_bwd):
        got_fwd, got_bwd = swap(
            tile_products(values_fwd, spread_fwd), tile_products(values_bwd, spread_bwd)
        )
        return place_rows(got_fwd, dst_placer), place_rows(got_bwd, dst_placer)

    far_fwd, far_bwd = push_hop(flat_hidden, flat_hidden)
    hop_fwd = (near_apply(flat_hidden, dense_fwd) + far_fwd).astype(jnp.bfloat16)
    hop_bwd = (near_apply(flat_hidden, dense_bwd) + far_bwd).astype(jnp.bfloat16)
    far_fwd, far_bwd = push_hop(hop_fwd, hop_bwd)
    two_fwd = (near_apply(hop_fwd, dense_fwd) + far_fwd).astype(jnp.bfloat16)
    two_bwd = (near_apply(hop_bwd, dense_bwd) + far_bwd).astype(jnp.bfloat16)
    stacked_parts = jnp.concatenate(
        [
            hidden,
            hop_fwd.reshape(shape4),
            two_fwd.reshape(shape4),
            hop_bwd.reshape(shape4),
            two_bwd.reshape(shape4),
        ],
        axis=2,
    )
    mixed_features = (
        jnp.einsum("oc,wtcn->wton", w_mix, stacked_parts, preferred_element_type=jnp.float32)
        + b_mix[None, None, :, None]
    )
    residual_stream = (inputs[:, DILATION_GAP:].astype(jnp.float32) + mixed_features).astype(
        jnp.bfloat16
    )
    last_step = hidden[:, output_steps - 1]
    skip_sum = (
        jnp.einsum("sc,wcn->wsn", w_skip, last_step, preferred_element_type=jnp.float32)
        + b_skip[None, :, None]
    ).astype(jnp.bfloat16)
    grad_parts = jnp.einsum(
        "co,wtcn->wton", w_mix, residual_cotangent, preferred_element_type=jnp.float32
    )
    grad_mix = jnp.einsum(
        "wtcn,wton->co", residual_cotangent, stacked_parts, preferred_element_type=jnp.float32
    )
    grad_bmix = jnp.sum(residual_cotangent.astype(jnp.float32), axis=(0, 1, 3))
    grad_skip = jnp.einsum("wsn,wcn->sc", cot_skip, last_step, preferred_element_type=jnp.float32)
    grad_bskip = jnp.sum(cot_skip.astype(jnp.float32), axis=(0, 2))

    def group_of(index):
        return grad_parts[:, :, index * channel_count : (index + 1) * channel_count].reshape(
            row_count, local_nodes
        )

    back2_fwd = group_of(2).astype(jnp.bfloat16)
    back2_bwd = group_of(4).astype(jnp.bfloat16)

    def fetch_rows(grad_fwd, grad_bwd):
        return swap(pick_rows(grad_fwd, dst_placer), pick_rows(grad_bwd, dst_placer))

    got_fwd, got_bwd = fetch_rows(back2_fwd, back2_bwd)
    near1_fwd = place_rows(tile_backward(got_fwd, remote_fwd).astype(jnp.bfloat16), src_placer)
    near1_bwd = place_rows(tile_backward(got_bwd, remote_bwd).astype(jnp.bfloat16), src_placer)
    back1_fwd = (group_of(1) + near_transpose(back2_fwd, dense_fwd) + near1_fwd).astype(
        jnp.bfloat16
    )
    back1_bwd = (group_of(3) + near_transpose(back2_bwd, dense_bwd) + near1_bwd).astype(
        jnp.bfloat16
    )
    got_fwd, got_bwd = fetch_rows(back1_fwd, back1_bwd)
    combined = (tile_backward(got_fwd, remote_fwd) + tile_backward(got_bwd, remote_bwd)).astype(
        jnp.bfloat16
    )
    far_total = place_rows(combined, src_placer)
    skip_back = jnp.einsum("sc,wsn->wcn", w_skip, cot_skip, preferred_element_type=jnp.float32)
    direct = (
        grad_parts[:, :, :channel_count]
        .at[:, output_steps - 1]
        .add(skip_back)
        .reshape(row_count, local_nodes)
    )
    summed = (
        direct
        + near_transpose(back1_fwd, dense_fwd)
        + near_transpose(back1_bwd, dense_bwd)
        + far_total
    )
    grad_hidden = summed.astype(jnp.bfloat16).reshape(shape4).astype(jnp.float32)
    grad_pre = jnp.concatenate(
        [
            grad_hidden * gate_val * (1.0 - filtered * filtered),
            grad_hidden * filtered * gate_val * (1.0 - gate_val),
        ],
        axis=2,
    ).astype(jnp.bfloat16)
    tap_gradients = jnp.einsum(
        "oc,wton->wtcn", w_conv, grad_pre, preferred_element_type=jnp.float32
    )
    input_gradient = jnp.zeros((windows, input_steps, channel_count, local_nodes), jnp.float32)
    input_gradient = input_gradient.at[:, :output_steps].add(tap_gradients[:, :, :channel_count])
    input_gradient = input_gradient.at[:, DILATION_GAP:].add(
        tap_gradients[:, :, channel_count:] + residual_cotangent.astype(jnp.float32)
    )
    grad_wconv = jnp.einsum(
        "wton,wtcn->oc", grad_pre, paired_taps, preferred_element_type=jnp.float32
    )
    grad_bconv = jnp.sum(grad_pre.astype(jnp.float32), axis=(0, 1, 3))
    totals = exchange_sum((grad_wconv, grad_bconv, grad_mix, grad_bmix, grad_skip, grad_bskip))
    grad_count = (
        windows * lax.axis_size("batch") * local_nodes * lax.axis_size("node") * output_steps
    )
    grad_scale = 1.0 / math.sqrt(float(grad_count))
    return (
        residual_stream,
        skip_sum,
        input_gradient.astype(jnp.bfloat16),
        totals[0] * grad_scale,
        totals[1] * grad_scale,
        totals[2] * grad_scale,
        totals[3] * grad_scale,
        totals[4] * grad_scale,
        totals[5] * grad_scale,
    )


def solution(mesh):
    return jax.shard_map(
        shards,
        mesh=mesh,
        in_specs=(
            P("batch", None, None, "node"),
            P(),
            P(),
            P(),
            P(),
            P(),
            P(),
            P("node", None),
            P("node", None),
            P("node", None, None),
            P("node", None, None),
            P("node"),
            P("node"),
            P("batch", None, None, "node"),
            P("batch", None, "node"),
        ),
        out_specs=(
            P("batch", None, None, "node"),
            P("batch", None, "node"),
            P("batch", None, None, "node"),
            P(),
            P(),
            P(),
            P(),
            P(),
            P(),
        ),
        check_vma=False,
    )
```

```python
import math

import jax
import jax.numpy as jnp
from jax import lax
from jax.sharding import PartitionSpec as P

DILATION_GAP = 2


def dense_band(weights, blocks, tile_width):
    shaped = weights.reshape(blocks, tile_width, 1, 3, tile_width)
    row_ids = lax.broadcasted_iota(jnp.int32, (blocks, 1, blocks, 3, 1), 0)
    col_ids = lax.broadcasted_iota(jnp.int32, (blocks, 1, blocks, 3, 1), 2)
    offsets = lax.broadcasted_iota(jnp.int32, (blocks, 1, blocks, 3, 1), 3)
    hits = (col_ids == row_ids + offsets - 1).astype(weights.dtype)
    placed = (shaped * hits).sum(axis=3, dtype=jnp.float32).astype(weights.dtype)
    return placed.reshape(blocks * tile_width, blocks * tile_width)


def spread_onehot(chooser, tile_vals):
    slots, blocks = chooser.shape
    tile_width = tile_vals.shape[2]
    placed = tile_vals[:, :, None, :] * chooser[:, None, :, None]
    return placed.reshape(slots, tile_vals.shape[1], blocks * tile_width)


def near_apply(values, dense):
    return jnp.einsum("mn,kn->mk", values, dense, preferred_element_type=jnp.float32)


def near_transpose(gradient, dense):
    return jnp.einsum("mk,kn->mn", gradient, dense, preferred_element_type=jnp.float32)


def tile_products(values, spread_tiles):
    return jnp.einsum(
        "mn,qan->qma", values, spread_tiles, preferred_element_type=jnp.float32
    ).astype(jnp.bfloat16)


def place_rows(pieces, placer):
    return jnp.einsum("sma,san->mn", pieces, placer, preferred_element_type=jnp.float32)


def pick_rows(values, placer):
    return jnp.einsum(
        "mn,san->sma", values, placer, preferred_element_type=jnp.float32
    ).astype(jnp.bfloat16)


def tile_backward(pieces, tile_vals):
    return jnp.einsum("qma,qac->qmc", pieces, tile_vals, preferred_element_type=jnp.float32)


def exchange_sum(pieces):
    sizes = [piece.size for piece in pieces]
    flat = jnp.concatenate([piece.reshape(-1) for piece in pieces])
    node_count = lax.axis_size("node")
    batch_count = lax.axis_size("batch")
    total = flat.shape[0]
    padded = -(-total // node_count) * node_count
    flat = jnp.pad(flat, (0, padded - total))
    part = lax.all_to_all(
        flat.reshape(node_count, padded // node_count), "node", 0, 0, tiled=True
    ).sum(axis=0)
    part = jnp.broadcast_to(part[None], (batch_count, padded // node_count))
    part = lax.all_to_all(part, "batch", 0, 0, tiled=True).sum(axis=0)
    spread = jnp.broadcast_to(part[None], (node_count, padded // node_count))
    spread = lax.all_to_all(spread, "node", 0, 0, tiled=True).reshape(padded)
    results = []
    offset = 0
    for piece, size in zip(pieces, sizes):
        results.append(spread[offset : offset + size].reshape(piece.shape))
        offset += size
    return tuple(results)


def shards(
    inputs,
    w_conv,
    b_conv,
    w_mix,
    b_mix,
    w_skip,
    b_skip,
    local_fwd,
    local_bwd,
    remote_fwd,
    remote_bwd,
    tile_src,
    tile_dst,
    residual_cotangent,
    cot_skip,
):
    windows, input_steps, channel_count, local_nodes = inputs.shape
    output_steps = input_steps - DILATION_GAP
    tile_width = remote_fwd.shape[1]
    blocks = local_nodes // tile_width
    block_ids = jnp.arange(blocks, dtype=jnp.int32)
    own_src = (tile_src[:, None] == block_ids[None, :]).astype(jnp.bfloat16)
    own_dst = (tile_dst[:, None] == block_ids[None, :]).astype(jnp.bfloat16)
    row_count = windows * output_steps * channel_count
    shape4 = (windows, output_steps, channel_count, local_nodes)
    paired_taps = jnp.concatenate([inputs[:, :output_steps], inputs[:, DILATION_GAP:]], axis=2)
    pre_act = (
        jnp.einsum("oc,wtcn->wton", w_conv, paired_taps, preferred_element_type=jnp.float32)
        + b_conv[None, None, :, None]
    )
    filtered = jnp.tanh(pre_act[:, :, :channel_count])
    gate_val = jax.nn.sigmoid(pre_act[:, :, channel_count:])
    hidden = (filtered * gate_val).astype(jnp.bfloat16)
    flat_hidden = hidden.reshape(row_count, local_nodes)
    eye_tile = jnp.eye(tile_width, dtype=jnp.bfloat16)
    eye_slots = jnp.broadcast_to(eye_tile, (own_src.shape[0], tile_width, tile_width))
    dense_fwd = dense_band(local_fwd, blocks, tile_width)
    dense_bwd = dense_band(local_bwd, blocks, tile_width)
    spread_fwd = spread_onehot(own_src, remote_fwd)
    spread_bwd = spread_onehot(own_src, remote_bwd)
    src_placer = spread_onehot(own_src, eye_slots)
    recv_dst = lax.all_to_all(own_dst, "node", split_axis=0, concat_axis=0, tiled=True)
    dst_placer = spread_onehot(recv_dst, eye_slots)

    def swap(pieces):
        got_all = lax.all_to_all(
            jnp.concatenate(pieces, axis=1), "node", split_axis=0, concat_axis=0, tiled=True
        )
        return [got_all[:, k * row_count : (k + 1) * row_count] for k in range(len(pieces))]

    grad_parts = jnp.einsum(
        "co,wtcn->wton", w_mix, residual_cotangent, preferred_element_type=jnp.float32
    )

    def group_of(index):
        return grad_parts[:, :, index * channel_count : (index + 1) * channel_count].reshape(
            row_count, local_nodes
        )

    back2_fwd = group_of(2).astype(jnp.bfloat16)
    back2_bwd = group_of(4).astype(jnp.bfloat16)

    got_fwd, got_bwd, got2_fwd, got2_bwd = swap(
        [
            tile_products(flat_hidden, spread_fwd),
            tile_products(flat_hidden, spread_bwd),
            pick_rows(back2_fwd, dst_placer),
            pick_rows(back2_bwd, dst_placer),
        ]
    )
    hop_fwd = (near_apply(flat_hidden, dense_fwd) + place_rows(got_fwd, dst_placer)).astype(
        jnp.bfloat16
    )
    hop_bwd = (near_apply(flat_hidden, dense_bwd) + place_rows(got_bwd, dst_placer)).astype(
        jnp.bfloat16
    )
    near1_fwd = place_rows(tile_backward(got2_fwd, remote_fwd).astype(jnp.bfloat16), src_placer)
    near1_bwd = place_rows(tile_backward(got2_bwd, remote_bwd).astype(jnp.bfloat16), src_placer)
    back1_fwd = (group_of(1) + near_transpose(back2_fwd, dense_fwd) + near1_fwd).astype(
        jnp.bfloat16
    )
    back1_bwd = (group_of(3) + near_transpose(back2_bwd, dense_bwd) + near1_bwd).astype(
        jnp.bfloat16
    )
    got_fwd, got_bwd, got1_fwd, got1_bwd = swap(
        [
            tile_products(hop_fwd, spread_fwd),
            tile_products(hop_bwd, spread_bwd),
            pick_rows(back1_fwd, dst_placer),
            pick_rows(back1_bwd, dst_placer),
        ]
    )
    two_fwd = (near_apply(hop_fwd, dense_fwd) + place_rows(got_fwd, dst_placer)).astype(
        jnp.bfloat16
    )
    two_bwd = (near_apply(hop_bwd, dense_bwd) + place_rows(got_bwd, dst_placer)).astype(
        jnp.bfloat16
    )
    combined = (tile_backward(got1_fwd, remote_fwd) + tile_backward(got1_bwd, remote_bwd)).astype(
        jnp.bfloat16
    )
    far_total = place_rows(combined, src_placer)
    stacked_parts = jnp.concatenate(
        [
            hidden,
            hop_fwd.reshape(shape4),
            two_fwd.reshape(shape4),
            hop_bwd.reshape(shape4),
            two_bwd.reshape(shape4),
        ],
        axis=2,
    )
    mixed_features = (
        jnp.einsum("oc,wtcn->wton", w_mix, stacked_parts, preferred_element_type=jnp.float32)
        + b_mix[None, None, :, None]
    )
    residual_stream = (inputs[:, DILATION_GAP:].astype(jnp.float32) + mixed_features).astype(
        jnp.bfloat16
    )
    last_step = hidden[:, output_steps - 1]
    skip_sum = (
        jnp.einsum("sc,wcn->wsn", w_skip, last_step, preferred_element_type=jnp.float32)
        + b_skip[None, :, None]
    ).astype(jnp.bfloat16)
    grad_mix = jnp.einsum(
        "wtcn,wton->co", residual_cotangent, stacked_parts, preferred_element_type=jnp.float32
    )
    grad_bmix = jnp.sum(residual_cotangent.astype(jnp.float32), axis=(0, 1, 3))
    grad_skip = jnp.einsum("wsn,wcn->sc", cot_skip, last_step, preferred_element_type=jnp.float32)
    grad_bskip = jnp.sum(cot_skip.astype(jnp.float32), axis=(0, 2))

    skip_back = jnp.einsum("sc,wsn->wcn", w_skip, cot_skip, preferred_element_type=jnp.float32)
    direct = (
        grad_parts[:, :, :channel_count]
        .at[:, output_steps - 1]
        .add(skip_back)
        .reshape(row_count, local_nodes)
    )
    summed = (
        direct
        + near_transpose(back1_fwd, dense_fwd)
        + near_transpose(back1_bwd, dense_bwd)
        + far_total
    )
    grad_hidden = summed.astype(jnp.bfloat16).reshape(shape4).astype(jnp.float32)
    grad_pre = jnp.concatenate(
        [
            grad_hidden * gate_val * (1.0 - filtered * filtered),
            grad_hidden * filtered * gate_val * (1.0 - gate_val),
        ],
        axis=2,
    ).astype(jnp.bfloat16)
    tap_gradients = jnp.einsum(
        "oc,wton->wtcn", w_conv, grad_pre, preferred_element_type=jnp.float32
    )
    input_gradient = jnp.zeros((windows, input_steps, channel_count, local_nodes), jnp.float32)
    input_gradient = input_gradient.at[:, :output_steps].add(tap_gradients[:, :, :channel_count])
    input_gradient = input_gradient.at[:, DILATION_GAP:].add(
        tap_gradients[:, :, channel_count:] + residual_cotangent.astype(jnp.float32)
    )
    grad_wconv = jnp.einsum(
        "wton,wtcn->oc", grad_pre, paired_taps, preferred_element_type=jnp.float32
    )
    grad_bconv = jnp.sum(grad_pre.astype(jnp.float32), axis=(0, 1, 3))
    totals = exchange_sum((grad_wconv, grad_bconv, grad_mix, grad_bmix, grad_skip, grad_bskip))
    grad_count = (
        windows * lax.axis_size("batch") * local_nodes * lax.axis_size("node") * output_steps
    )
    grad_scale = 1.0 / math.sqrt(float(grad_count))
    return (
        residual_stream,
        skip_sum,
        input_gradient.astype(jnp.bfloat16),
        totals[0] * grad_scale,
        totals[1] * grad_scale,
        totals[2] * grad_scale,
        totals[3] * grad_scale,
        totals[4] * grad_scale,
        totals[5] * grad_scale,
    )


def solution(mesh):
    return jax.shard_map(
        shards,
        mesh=mesh,
        in_specs=(
            P("batch", None, None, "node"),
            P(),
            P(),
            P(),
            P(),
            P(),
            P(),
            P("node", None),
            P("node", None),
            P("node", None, None),
            P("node", None, None),
            P("node"),
            P("node"),
            P("batch", None, None, "node"),
            P("batch", None, "node"),
        ),
        out_specs=(
            P("batch", None, None, "node"),
            P("batch", None, "node"),
            P("batch", None, None, "node"),
            P(),
            P(),
            P(),
            P(),
            P(),
            P(),
        ),
        check_vma=False,
    )
```

```python
import math

import jax
import jax.numpy as jnp
from jax import lax
from jax.sharding import PartitionSpec as P

DILATION_GAP = 2


def dense_band(weights, blocks, tile_width):
    shaped = weights.reshape(blocks, tile_width, 1, 3, tile_width)
    row_ids = lax.broadcasted_iota(jnp.int32, (blocks, 1, blocks, 3, 1), 0)
    col_ids = lax.broadcasted_iota(jnp.int32, (blocks, 1, blocks, 3, 1), 2)
    offsets = lax.broadcasted_iota(jnp.int32, (blocks, 1, blocks, 3, 1), 3)
    hits = (col_ids == row_ids + offsets - 1).astype(weights.dtype)
    placed = (shaped * hits).sum(axis=3, dtype=jnp.float32).astype(weights.dtype)
    return placed.reshape(blocks * tile_width, blocks * tile_width)


def spread_onehot(chooser, tile_vals):
    slots, blocks = chooser.shape
    tile_width = tile_vals.shape[2]
    placed = tile_vals[:, :, None, :] * chooser[:, None, :, None]
    return placed.reshape(slots, tile_vals.shape[1], blocks * tile_width)


def near_apply(values, dense):
    return jnp.einsum("mn,kn->mk", values, dense, preferred_element_type=jnp.float32)


def near_transpose(gradient, dense):
    return jnp.einsum("mk,kn->mn", gradient, dense, preferred_element_type=jnp.float32)


def place_rows(pieces, placer):
    return jnp.einsum("sma,san->mn", pieces, placer, preferred_element_type=jnp.float32)


def pick_rows(values, placer):
    return jnp.einsum(
        "mn,san->sma", values, placer, preferred_element_type=jnp.float32
    ).astype(jnp.bfloat16)


def exchange_sum(pieces):
    sizes = [piece.size for piece in pieces]
    flat = jnp.concatenate([piece.reshape(-1) for piece in pieces])
    node_count = lax.axis_size("node")
    batch_count = lax.axis_size("batch")
    total = flat.shape[0]
    padded = -(-total // node_count) * node_count
    flat = jnp.pad(flat, (0, padded - total))
    part = lax.all_to_all(
        flat.reshape(node_count, padded // node_count), "node", 0, 0, tiled=True
    ).sum(axis=0)
    part = jnp.broadcast_to(part[None], (batch_count, padded // node_count))
    part = lax.all_to_all(part, "batch", 0, 0, tiled=True).sum(axis=0)
    spread = jnp.broadcast_to(part[None], (node_count, padded // node_count))
    spread = lax.all_to_all(spread, "node", 0, 0, tiled=True).reshape(padded)
    results = []
    offset = 0
    for piece, size in zip(pieces, sizes):
        results.append(spread[offset : offset + size].reshape(piece.shape))
        offset += size
    return tuple(results)


def shards(
    inputs,
    w_conv,
    b_conv,
    w_mix,
    b_mix,
    w_skip,
    b_skip,
    local_fwd,
    local_bwd,
    remote_fwd,
    remote_bwd,
    tile_src,
    tile_dst,
    residual_cotangent,
    cot_skip,
):
    windows, input_steps, channel_count, local_nodes = inputs.shape
    output_steps = input_steps - DILATION_GAP
    tile_width = remote_fwd.shape[1]
    blocks = local_nodes // tile_width
    block_ids = jnp.arange(blocks, dtype=jnp.int32)
    own_src = (tile_src[:, None] == block_ids[None, :]).astype(jnp.bfloat16)
    own_dst = (tile_dst[:, None] == block_ids[None, :]).astype(jnp.bfloat16)
    row_count = windows * output_steps * channel_count
    shape4 = (windows, output_steps, channel_count, local_nodes)
    paired_taps = jnp.concatenate([inputs[:, :output_steps], inputs[:, DILATION_GAP:]], axis=2)
    pre_act = (
        jnp.einsum("oc,wtcn->wton", w_conv, paired_taps, preferred_element_type=jnp.float32)
        + b_conv[None, None, :, None]
    )
    filtered = jnp.tanh(pre_act[:, :, :channel_count])
    gate_val = jax.nn.sigmoid(pre_act[:, :, channel_count:])
    hidden = (filtered * gate_val).astype(jnp.bfloat16)
    flat_hidden = hidden.reshape(row_count, local_nodes)
    eye_tile = jnp.eye(tile_width, dtype=jnp.bfloat16)
    eye_slots = jnp.broadcast_to(eye_tile, (own_src.shape[0], tile_width, tile_width))
    dense_fwd = dense_band(local_fwd, blocks, tile_width)
    dense_bwd = dense_band(local_bwd, blocks, tile_width)
    src_placer = spread_onehot(own_src, eye_slots)
    recv_dst = lax.all_to_all(own_dst, "node", split_axis=0, concat_axis=0, tiled=True)
    dst_placer = spread_onehot(recv_dst, eye_slots)
    tiles_in = lax.all_to_all(
        jnp.concatenate([remote_fwd, remote_bwd], axis=1),
        "node",
        split_axis=0,
        concat_axis=0,
        tiled=True,
    )
    tiles_fwd, tiles_bwd = tiles_in[:, :tile_width], tiles_in[:, tile_width:]

    def swap(pieces):
        got_all = lax.all_to_all(
            jnp.concatenate(pieces, axis=1), "node", split_axis=0, concat_axis=0, tiled=True
        )
        return [got_all[:, k * row_count : (k + 1) * row_count] for k in range(len(pieces))]

    def far_terms(columns, tiles):
        return jnp.einsum(
            "smc,sac->sma", columns, tiles, preferred_element_type=jnp.float32
        ).astype(jnp.bfloat16)

    def row_terms(gradient, tiles):
        wanted = pick_rows(gradient, dst_placer)
        return jnp.einsum("sma,sac->smc", wanted, tiles, preferred_element_type=jnp.float32)

    (columns,) = swap([pick_rows(flat_hidden, src_placer)])
    far_fwd = place_rows(far_terms(columns, tiles_fwd), dst_placer)
    far_bwd = place_rows(far_terms(columns, tiles_bwd), dst_placer)
    hop_fwd = (near_apply(flat_hidden, dense_fwd) + far_fwd).astype(jnp.bfloat16)
    hop_bwd = (near_apply(flat_hidden, dense_bwd) + far_bwd).astype(jnp.bfloat16)
    columns_fwd, columns_bwd = swap(
        [pick_rows(hop_fwd, src_placer), pick_rows(hop_bwd, src_placer)]
    )
    far_fwd = place_rows(far_terms(columns_fwd, tiles_fwd), dst_placer)
    far_bwd = place_rows(far_terms(columns_bwd, tiles_bwd), dst_placer)
    two_fwd = (near_apply(hop_fwd, dense_fwd) + far_fwd).astype(jnp.bfloat16)
    two_bwd = (near_apply(hop_bwd, dense_bwd) + far_bwd).astype(jnp.bfloat16)
    stacked_parts = jnp.concatenate(
        [
            hidden,
            hop_fwd.reshape(shape4),
            two_fwd.reshape(shape4),
            hop_bwd.reshape(shape4),
            two_bwd.reshape(shape4),
        ],
        axis=2,
    )
    mixed_features = (
        jnp.einsum("oc,wtcn->wton", w_mix, stacked_parts, preferred_element_type=jnp.float32)
        + b_mix[None, None, :, None]
    )
    residual_stream = (inputs[:, DILATION_GAP:].astype(jnp.float32) + mixed_features).astype(
        jnp.bfloat16
    )
    last_step = hidden[:, output_steps - 1]
    skip_sum = (
        jnp.einsum("sc,wcn->wsn", w_skip, last_step, preferred_element_type=jnp.float32)
        + b_skip[None, :, None]
    ).astype(jnp.bfloat16)
    grad_parts = jnp.einsum(
        "co,wtcn->wton", w_mix, residual_cotangent, preferred_element_type=jnp.float32
    )
    grad_mix = jnp.einsum(
        "wtcn,wton->co", residual_cotangent, stacked_parts, preferred_element_type=jnp.float32
    )
    grad_bmix = jnp.sum(residual_cotangent.astype(jnp.float32), axis=(0, 1, 3))
    grad_skip = jnp.einsum("wsn,wcn->sc", cot_skip, last_step, preferred_element_type=jnp.float32)
    grad_bskip = jnp.sum(cot_skip.astype(jnp.float32), axis=(0, 2))

    def group_of(index):
        return grad_parts[:, :, index * channel_count : (index + 1) * channel_count].reshape(
            row_count, local_nodes
        )

    back2_fwd = group_of(2).astype(jnp.bfloat16)
    back2_bwd = group_of(4).astype(jnp.bfloat16)

    got_fwd, got_bwd = swap(
        [
            row_terms(back2_fwd, tiles_fwd).astype(jnp.bfloat16),
            row_terms(back2_bwd, tiles_bwd).astype(jnp.bfloat16),
        ]
    )
    near1_fwd = place_rows(got_fwd, src_placer)
    near1_bwd = place_rows(got_bwd, src_placer)
    back1_fwd = (group_of(1) + near_transpose(back2_fwd, dense_fwd) + near1_fwd).astype(
        jnp.bfloat16
    )
    back1_bwd = (group_of(3) + near_transpose(back2_bwd, dense_bwd) + near1_bwd).astype(
        jnp.bfloat16
    )
    (combined,) = swap(
        [(row_terms(back1_fwd, tiles_fwd) + row_terms(back1_bwd, tiles_bwd)).astype(jnp.bfloat16)]
    )
    far_total = place_rows(combined, src_placer)
    skip_back = jnp.einsum("sc,wsn->wcn", w_skip, cot_skip, preferred_element_type=jnp.float32)
    direct = (
        grad_parts[:, :, :channel_count]
        .at[:, output_steps - 1]
        .add(skip_back)
        .reshape(row_count, local_nodes)
    )
    summed = (
        direct
        + near_transpose(back1_fwd, dense_fwd)
        + near_transpose(back1_bwd, dense_bwd)
        + far_total
    )
    grad_hidden = summed.astype(jnp.bfloat16).reshape(shape4).astype(jnp.float32)
    grad_pre = jnp.concatenate(
        [
            grad_hidden * gate_val * (1.0 - filtered * filtered),
            grad_hidden * filtered * gate_val * (1.0 - gate_val),
        ],
        axis=2,
    ).astype(jnp.bfloat16)
    tap_gradients = jnp.einsum(
        "oc,wton->wtcn", w_conv, grad_pre, preferred_element_type=jnp.float32
    )
    input_gradient = jnp.zeros((windows, input_steps, channel_count, local_nodes), jnp.float32)
    input_gradient = input_gradient.at[:, :output_steps].add(tap_gradients[:, :, :channel_count])
    input_gradient = input_gradient.at[:, DILATION_GAP:].add(
        tap_gradients[:, :, channel_count:] + residual_cotangent.astype(jnp.float32)
    )
    grad_wconv = jnp.einsum(
        "wton,wtcn->oc", grad_pre, paired_taps, preferred_element_type=jnp.float32
    )
    grad_bconv = jnp.sum(grad_pre.astype(jnp.float32), axis=(0, 1, 3))
    totals = exchange_sum((grad_wconv, grad_bconv, grad_mix, grad_bmix, grad_skip, grad_bskip))
    grad_count = (
        windows * lax.axis_size("batch") * local_nodes * lax.axis_size("node") * output_steps
    )
    grad_scale = 1.0 / math.sqrt(float(grad_count))
    return (
        residual_stream,
        skip_sum,
        input_gradient.astype(jnp.bfloat16),
        totals[0] * grad_scale,
        totals[1] * grad_scale,
        totals[2] * grad_scale,
        totals[3] * grad_scale,
        totals[4] * grad_scale,
        totals[5] * grad_scale,
    )


def solution(mesh):
    return jax.shard_map(
        shards,
        mesh=mesh,
        in_specs=(
            P("batch", None, None, "node"),
            P(),
            P(),
            P(),
            P(),
            P(),
            P(),
            P("node", None),
            P("node", None),
            P("node", None, None),
            P("node", None, None),
            P("node"),
            P("node"),
            P("batch", None, None, "node"),
            P("batch", None, "node"),
        ),
        out_specs=(
            P("batch", None, None, "node"),
            P("batch", None, "node"),
            P("batch", None, None, "node"),
            P(),
            P(),
            P(),
            P(),
            P(),
            P(),
        ),
        check_vma=False,
    )
```

```python
import math

import jax
import jax.numpy as jnp
from jax import lax
from jax.sharding import PartitionSpec as P

DILATION_GAP = 2


def dense_band(weights, blocks, tile_width):
    shaped = weights.reshape(blocks, tile_width, 1, 3, tile_width)
    row_ids = lax.broadcasted_iota(jnp.int32, (blocks, 1, blocks, 3, 1), 0)
    col_ids = lax.broadcasted_iota(jnp.int32, (blocks, 1, blocks, 3, 1), 2)
    offsets = lax.broadcasted_iota(jnp.int32, (blocks, 1, blocks, 3, 1), 3)
    hits = (col_ids == row_ids + offsets - 1).astype(weights.dtype)
    placed = (shaped * hits).sum(axis=3, dtype=jnp.float32).astype(weights.dtype)
    return placed.reshape(blocks * tile_width, blocks * tile_width)


def spread_onehot(chooser, tile_vals):
    slots, blocks = chooser.shape
    tile_width = tile_vals.shape[2]
    placed = tile_vals[:, :, None, :] * chooser[:, None, :, None]
    return placed.reshape(slots, tile_vals.shape[1], blocks * tile_width)


def near_apply(values, dense):
    return jnp.einsum("mn,kn->mk", values, dense, preferred_element_type=jnp.float32)


def near_transpose(gradient, dense):
    return jnp.einsum("mk,kn->mn", gradient, dense, preferred_element_type=jnp.float32)


def place_rows(pieces, placer):
    return jnp.einsum("sma,san->mn", pieces, placer, preferred_element_type=jnp.float32)


def pick_rows(values, placer):
    return jnp.einsum(
        "mn,san->sma", values, placer, preferred_element_type=jnp.float32
    ).astype(jnp.bfloat16)


def exchange_sum(pieces):
    sizes = [piece.size for piece in pieces]
    flat = jnp.concatenate([piece.reshape(-1) for piece in pieces])
    node_count = lax.axis_size("node")
    batch_count = lax.axis_size("batch")
    total = flat.shape[0]
    padded = -(-total // node_count) * node_count
    flat = jnp.pad(flat, (0, padded - total))
    part = lax.all_to_all(
        flat.reshape(node_count, padded // node_count), "node", 0, 0, tiled=True
    ).sum(axis=0)
    part = jnp.broadcast_to(part[None], (batch_count, padded // node_count))
    part = lax.all_to_all(part, "batch", 0, 0, tiled=True).sum(axis=0)
    spread = jnp.broadcast_to(part[None], (node_count, padded // node_count))
    spread = lax.all_to_all(spread, "node", 0, 0, tiled=True).reshape(padded)
    results = []
    offset = 0
    for piece, size in zip(pieces, sizes):
        results.append(spread[offset : offset + size].reshape(piece.shape))
        offset += size
    return tuple(results)


def shards(
    inputs,
    w_conv,
    b_conv,
    w_mix,
    b_mix,
    w_skip,
    b_skip,
    local_fwd,
    local_bwd,
    remote_fwd,
    remote_bwd,
    tile_src,
    tile_dst,
    residual_cotangent,
    cot_skip,
):
    windows, input_steps, channel_count, local_nodes = inputs.shape
    output_steps = input_steps - DILATION_GAP
    tile_width = remote_fwd.shape[1]
    blocks = local_nodes // tile_width
    block_ids = jnp.arange(blocks, dtype=jnp.int32)
    own_src = (tile_src[:, None] == block_ids[None, :]).astype(jnp.bfloat16)
    own_dst = (tile_dst[:, None] == block_ids[None, :]).astype(jnp.bfloat16)
    row_count = windows * output_steps * channel_count
    shape4 = (windows, output_steps, channel_count, local_nodes)
    paired_taps = jnp.concatenate([inputs[:, :output_steps], inputs[:, DILATION_GAP:]], axis=2)
    pre_act = (
        jnp.einsum("oc,wtcn->wton", w_conv, paired_taps, preferred_element_type=jnp.float32)
        + b_conv[None, None, :, None]
    )
    filtered = jnp.tanh(pre_act[:, :, :channel_count])
    gate_val = jax.nn.sigmoid(pre_act[:, :, channel_count:])
    hidden = (filtered * gate_val).astype(jnp.bfloat16)
    flat_hidden = hidden.reshape(row_count, local_nodes)
    eye_tile = jnp.eye(tile_width, dtype=jnp.bfloat16)
    eye_slots = jnp.broadcast_to(eye_tile, (own_src.shape[0], tile_width, tile_width))
    dense_fwd = dense_band(local_fwd, blocks, tile_width)
    dense_bwd = dense_band(local_bwd, blocks, tile_width)
    src_placer = spread_onehot(own_src, eye_slots)
    recv_dst = lax.all_to_all(own_dst, "node", split_axis=0, concat_axis=0, tiled=True)
    dst_placer = spread_onehot(recv_dst, eye_slots)
    tiles_in = lax.all_to_all(
        jnp.concatenate([remote_fwd, remote_bwd], axis=1),
        "node",
        split_axis=0,
        concat_axis=0,
        tiled=True,
    )
    tiles_fwd, tiles_bwd = tiles_in[:, :tile_width], tiles_in[:, tile_width:]
    slot_count = own_src.shape[0]

    def swap(pieces):
        got_all = lax.all_to_all(
            jnp.concatenate(pieces, axis=1), "node", split_axis=0, concat_axis=0, tiled=True
        )
        return [got_all[:, k * row_count : (k + 1) * row_count] for k in range(len(pieces))]

    def far_terms(columns, tiles):
        return jnp.einsum(
            "smc,sac->sma", columns, tiles, preferred_element_type=jnp.float32
        ).astype(jnp.bfloat16)

    row_tiles = jnp.stack(
        [
            (tiles_fwd[:, None] * recv_dst[:, :, None, None]).reshape(
                slot_count, local_nodes, tile_width
            ),
            (tiles_bwd[:, None] * recv_dst[:, :, None, None]).reshape(
                slot_count, local_nodes, tile_width
            ),
        ]
    )

    def row_terms(gradient_fwd, gradient_bwd):
        return jnp.einsum(
            "dmn,dsnc->sdmc",
            jnp.stack([gradient_fwd, gradient_bwd]),
            row_tiles,
            preferred_element_type=jnp.float32,
        ).astype(jnp.bfloat16)

    def row_terms_summed(gradient_fwd, gradient_bwd):
        return jnp.einsum(
            "dmn,dsnc->smc",
            jnp.stack([gradient_fwd, gradient_bwd]),
            row_tiles,
            preferred_element_type=jnp.float32,
        ).astype(jnp.bfloat16)

    def exchange(send):
        return lax.all_to_all(send, "node", split_axis=0, concat_axis=0, tiled=True)

    (columns,) = swap([pick_rows(flat_hidden, src_placer)])
    far_fwd = place_rows(far_terms(columns, tiles_fwd), dst_placer)
    far_bwd = place_rows(far_terms(columns, tiles_bwd), dst_placer)
    hop_fwd = (near_apply(flat_hidden, dense_fwd) + far_fwd).astype(jnp.bfloat16)
    hop_bwd = (near_apply(flat_hidden, dense_bwd) + far_bwd).astype(jnp.bfloat16)
    columns_both = exchange(
        jnp.einsum(
            "dmn,scn->sdmc",
            jnp.stack([hop_fwd, hop_bwd]),
            src_placer,
            preferred_element_type=jnp.float32,
        )
        .astype(jnp.bfloat16)
        .reshape(slot_count, 2 * row_count, tile_width)
    )
    columns_fwd, columns_bwd = columns_both[:, :row_count], columns_both[:, row_count:]
    far_fwd = place_rows(far_terms(columns_fwd, tiles_fwd), dst_placer)
    far_bwd = place_rows(far_terms(columns_bwd, tiles_bwd), dst_placer)
    two_fwd = (near_apply(hop_fwd, dense_fwd) + far_fwd).astype(jnp.bfloat16)
    two_bwd = (near_apply(hop_bwd, dense_bwd) + far_bwd).astype(jnp.bfloat16)
    stacked_parts = jnp.concatenate(
        [
            hidden,
            hop_fwd.reshape(shape4),
            two_fwd.reshape(shape4),
            hop_bwd.reshape(shape4),
            two_bwd.reshape(shape4),
        ],
        axis=2,
    )
    mixed_features = (
        jnp.einsum("oc,wtcn->wton", w_mix, stacked_parts, preferred_element_type=jnp.float32)
        + b_mix[None, None, :, None]
    )
    residual_stream = (inputs[:, DILATION_GAP:].astype(jnp.float32) + mixed_features).astype(
        jnp.bfloat16
    )
    last_step = hidden[:, output_steps - 1]
    skip_sum = (
        jnp.einsum("sc,wcn->wsn", w_skip, last_step, preferred_element_type=jnp.float32)
        + b_skip[None, :, None]
    ).astype(jnp.bfloat16)
    grad_parts = jnp.einsum(
        "co,wtcn->wton", w_mix, residual_cotangent, preferred_element_type=jnp.float32
    )
    grad_mix = jnp.einsum(
        "wtcn,wton->co", residual_cotangent, stacked_parts, preferred_element_type=jnp.float32
    )
    grad_bmix = jnp.sum(residual_cotangent.astype(jnp.float32), axis=(0, 1, 3))
    grad_skip = jnp.einsum("wsn,wcn->sc", cot_skip, last_step, preferred_element_type=jnp.float32)
    grad_bskip = jnp.sum(cot_skip.astype(jnp.float32), axis=(0, 2))

    def group_of(index):
        return grad_parts[:, :, index * channel_count : (index + 1) * channel_count].reshape(
            row_count, local_nodes
        )

    back2_fwd = group_of(2).astype(jnp.bfloat16)
    back2_bwd = group_of(4).astype(jnp.bfloat16)

    got_both = exchange(
        row_terms(back2_fwd, back2_bwd).reshape(slot_count, 2 * row_count, tile_width)
    )
    got_fwd, got_bwd = got_both[:, :row_count], got_both[:, row_count:]
    near1_fwd = place_rows(got_fwd, src_placer)
    near1_bwd = place_rows(got_bwd, src_placer)
    back1_fwd = (group_of(1) + near_transpose(back2_fwd, dense_fwd) + near1_fwd).astype(
        jnp.bfloat16
    )
    back1_bwd = (group_of(3) + near_transpose(back2_bwd, dense_bwd) + near1_bwd).astype(
        jnp.bfloat16
    )
    combined = exchange(row_terms_summed(back1_fwd, back1_bwd))
    far_total = place_rows(combined, src_placer)
    skip_back = jnp.einsum("sc,wsn->wcn", w_skip, cot_skip, preferred_element_type=jnp.float32)
    direct = (
        grad_parts[:, :, :channel_count]
        .at[:, output_steps - 1]
        .add(skip_back)
        .reshape(row_count, local_nodes)
    )
    summed = (
        direct
        + near_transpose(back1_fwd, dense_fwd)
        + near_transpose(back1_bwd, dense_bwd)
        + far_total
    )
    grad_hidden = summed.astype(jnp.bfloat16).reshape(shape4).astype(jnp.float32)
    grad_pre = jnp.concatenate(
        [
            grad_hidden * gate_val * (1.0 - filtered * filtered),
            grad_hidden * filtered * gate_val * (1.0 - gate_val),
        ],
        axis=2,
    ).astype(jnp.bfloat16)
    tap_gradients = jnp.einsum(
        "oc,wton->wtcn", w_conv, grad_pre, preferred_element_type=jnp.float32
    )
    input_gradient = jnp.zeros((windows, input_steps, channel_count, local_nodes), jnp.float32)
    input_gradient = input_gradient.at[:, :output_steps].add(tap_gradients[:, :, :channel_count])
    input_gradient = input_gradient.at[:, DILATION_GAP:].add(
        tap_gradients[:, :, channel_count:] + residual_cotangent.astype(jnp.float32)
    )
    grad_wconv = jnp.einsum(
        "wton,wtcn->oc", grad_pre, paired_taps, preferred_element_type=jnp.float32
    )
    grad_bconv = jnp.sum(grad_pre.astype(jnp.float32), axis=(0, 1, 3))
    totals = exchange_sum((grad_wconv, grad_bconv, grad_mix, grad_bmix, grad_skip, grad_bskip))
    grad_count = (
        windows * lax.axis_size("batch") * local_nodes * lax.axis_size("node") * output_steps
    )
    grad_scale = 1.0 / math.sqrt(float(grad_count))
    return (
        residual_stream,
        skip_sum,
        input_gradient.astype(jnp.bfloat16),
        totals[0] * grad_scale,
        totals[1] * grad_scale,
        totals[2] * grad_scale,
        totals[3] * grad_scale,
        totals[4] * grad_scale,
        totals[5] * grad_scale,
    )


def solution(mesh):
    return jax.shard_map(
        shards,
        mesh=mesh,
        in_specs=(
            P("batch", None, None, "node"),
            P(),
            P(),
            P(),
            P(),
            P(),
            P(),
            P("node", None),
            P("node", None),
            P("node", None, None),
            P("node", None, None),
            P("node"),
            P("node"),
            P("batch", None, None, "node"),
            P("batch", None, "node"),
        ),
        out_specs=(
            P("batch", None, None, "node"),
            P("batch", None, "node"),
            P("batch", None, None, "node"),
            P(),
            P(),
            P(),
            P(),
            P(),
            P(),
        ),
        check_vma=False,
    )
```

```python
import math

import jax
import jax.numpy as jnp
from jax import lax
from jax.sharding import PartitionSpec as P

DILATION_GAP = 2


def dense_band(weights, blocks, tile_width):
    shaped = weights.reshape(blocks, tile_width, 1, 3, tile_width)
    row_ids = lax.broadcasted_iota(jnp.int32, (blocks, 1, blocks, 3, 1), 0)
    col_ids = lax.broadcasted_iota(jnp.int32, (blocks, 1, blocks, 3, 1), 2)
    offsets = lax.broadcasted_iota(jnp.int32, (blocks, 1, blocks, 3, 1), 3)
    hits = (col_ids == row_ids + offsets - 1).astype(weights.dtype)
    placed = (shaped * hits).sum(axis=3, dtype=jnp.float32).astype(weights.dtype)
    return placed.reshape(blocks * tile_width, blocks * tile_width)


def spread_onehot(chooser, tile_vals):
    slots, blocks = chooser.shape
    tile_width = tile_vals.shape[2]
    placed = tile_vals[:, :, None, :] * chooser[:, None, :, None]
    return placed.reshape(slots, tile_vals.shape[1], blocks * tile_width)


def near_apply(values, dense):
    return jnp.einsum("mn,kn->mk", values, dense, preferred_element_type=jnp.float32)


def near_transpose(gradient, dense):
    return jnp.einsum("mk,kn->mn", gradient, dense, preferred_element_type=jnp.float32)


def place_rows(pieces, placer):
    return jnp.einsum("sma,san->mn", pieces, placer, preferred_element_type=jnp.float32)


def pick_rows(values, placer):
    return jnp.einsum(
        "mn,san->sma", values, placer, preferred_element_type=jnp.float32
    ).astype(jnp.bfloat16)


def exchange_sum(pieces):
    sizes = [piece.size for piece in pieces]
    flat = jnp.concatenate([piece.reshape(-1) for piece in pieces])
    node_count = lax.axis_size("node")
    batch_count = lax.axis_size("batch")
    total = flat.shape[0]
    padded = -(-total // node_count) * node_count
    flat = jnp.pad(flat, (0, padded - total))
    part = lax.all_to_all(
        flat.reshape(node_count, padded // node_count), "node", 0, 0, tiled=True
    ).sum(axis=0)
    part = jnp.broadcast_to(part[None], (batch_count, padded // node_count))
    part = lax.all_to_all(part, "batch", 0, 0, tiled=True).sum(axis=0)
    spread = jnp.broadcast_to(part[None], (node_count, padded // node_count))
    spread = lax.all_to_all(spread, "node", 0, 0, tiled=True).reshape(padded)
    results = []
    offset = 0
    for piece, size in zip(pieces, sizes):
        results.append(spread[offset : offset + size].reshape(piece.shape))
        offset += size
    return tuple(results)


def shards(
    inputs,
    w_conv,
    b_conv,
    w_mix,
    b_mix,
    w_skip,
    b_skip,
    local_fwd,
    local_bwd,
    remote_fwd,
    remote_bwd,
    tile_src,
    tile_dst,
    residual_cotangent,
    cot_skip,
):
    windows, input_steps, channel_count, local_nodes = inputs.shape
    output_steps = input_steps - DILATION_GAP
    tile_width = remote_fwd.shape[1]
    blocks = local_nodes // tile_width
    block_ids = jnp.arange(blocks, dtype=jnp.int32)
    own_src = (tile_src[:, None] == block_ids[None, :]).astype(jnp.bfloat16)
    own_dst = (tile_dst[:, None] == block_ids[None, :]).astype(jnp.bfloat16)
    row_count = windows * output_steps * channel_count
    shape4 = (windows, output_steps, channel_count, local_nodes)
    paired_taps = jnp.concatenate([inputs[:, :output_steps], inputs[:, DILATION_GAP:]], axis=2)
    pre_act = (
        jnp.einsum("oc,wtcn->wton", w_conv, paired_taps, preferred_element_type=jnp.float32)
        + b_conv[None, None, :, None]
    )
    filtered = jnp.tanh(pre_act[:, :, :channel_count])
    gate_val = jax.nn.sigmoid(pre_act[:, :, channel_count:])
    hidden = (filtered * gate_val).astype(jnp.bfloat16)
    flat_hidden = hidden.reshape(row_count, local_nodes)
    eye_tile = jnp.eye(tile_width, dtype=jnp.bfloat16)
    eye_slots = jnp.broadcast_to(eye_tile, (own_src.shape[0], tile_width, tile_width))
    dense_fwd = dense_band(local_fwd, blocks, tile_width)
    dense_bwd = dense_band(local_bwd, blocks, tile_width)
    src_placer = spread_onehot(own_src, eye_slots)
    dst_rows = jnp.zeros((own_dst.shape[0], 8, tile_width), jnp.bfloat16)
    dst_rows = dst_rows.at[:, 0, :blocks].set(own_dst)
    tiles_in = lax.all_to_all(
        jnp.concatenate([remote_fwd, remote_bwd, dst_rows], axis=1),
        "node",
        split_axis=0,
        concat_axis=0,
        tiled=True,
    )
    recv_dst = tiles_in[:, 2 * tile_width, :blocks]
    dst_placer = spread_onehot(recv_dst, eye_slots)
    tiles_fwd, tiles_bwd = tiles_in[:, :tile_width], tiles_in[:, tile_width : 2 * tile_width]

    def swap(pieces):
        got_all = lax.all_to_all(
            jnp.concatenate(pieces, axis=1), "node", split_axis=0, concat_axis=0, tiled=True
        )
        return [got_all[:, k * row_count : (k + 1) * row_count] for k in range(len(pieces))]

    def far_terms(columns, tiles):
        return jnp.einsum(
            "smc,sac->sma", columns, tiles, preferred_element_type=jnp.float32
        ).astype(jnp.bfloat16)

    def row_terms(gradient, tiles):
        wanted = pick_rows(gradient, dst_placer)
        return jnp.einsum("sma,sac->smc", wanted, tiles, preferred_element_type=jnp.float32)

    (columns,) = swap([pick_rows(flat_hidden, src_placer)])
    far_fwd = place_rows(far_terms(columns, tiles_fwd), dst_placer)
    far_bwd = place_rows(far_terms(columns, tiles_bwd), dst_placer)
    hop_fwd = (near_apply(flat_hidden, dense_fwd) + far_fwd).astype(jnp.bfloat16)
    hop_bwd = (near_apply(flat_hidden, dense_bwd) + far_bwd).astype(jnp.bfloat16)
    columns_fwd, columns_bwd = swap(
        [pick_rows(hop_fwd, src_placer), pick_rows(hop_bwd, src_placer)]
    )
    far_fwd = place_rows(far_terms(columns_fwd, tiles_fwd), dst_placer)
    far_bwd = place_rows(far_terms(columns_bwd, tiles_bwd), dst_placer)
    two_fwd = (near_apply(hop_fwd, dense_fwd) + far_fwd).astype(jnp.bfloat16)
    two_bwd = (near_apply(hop_bwd, dense_bwd) + far_bwd).astype(jnp.bfloat16)
    stacked_parts = jnp.concatenate(
        [
            hidden,
            hop_fwd.reshape(shape4),
            two_fwd.reshape(shape4),
            hop_bwd.reshape(shape4),
            two_bwd.reshape(shape4),
        ],
        axis=2,
    )
    mixed_features = (
        jnp.einsum("oc,wtcn->wton", w_mix, stacked_parts, preferred_element_type=jnp.float32)
        + b_mix[None, None, :, None]
    )
    residual_stream = (inputs[:, DILATION_GAP:].astype(jnp.float32) + mixed_features).astype(
        jnp.bfloat16
    )
    last_step = hidden[:, output_steps - 1]
    skip_sum = (
        jnp.einsum("sc,wcn->wsn", w_skip, last_step, preferred_element_type=jnp.float32)
        + b_skip[None, :, None]
    ).astype(jnp.bfloat16)
    grad_parts = jnp.einsum(
        "co,wtcn->wton", w_mix, residual_cotangent, preferred_element_type=jnp.float32
    )
    grad_mix = jnp.einsum(
        "wtcn,wton->co", residual_cotangent, stacked_parts, preferred_element_type=jnp.float32
    )
    grad_bmix = jnp.sum(residual_cotangent.astype(jnp.float32), axis=(0, 1, 3))
    grad_skip = jnp.einsum("wsn,wcn->sc", cot_skip, last_step, preferred_element_type=jnp.float32)
    grad_bskip = jnp.sum(cot_skip.astype(jnp.float32), axis=(0, 2))

    def group_of(index):
        return grad_parts[:, :, index * channel_count : (index + 1) * channel_count].reshape(
            row_count, local_nodes
        )

    back2_fwd = group_of(2).astype(jnp.bfloat16)
    back2_bwd = group_of(4).astype(jnp.bfloat16)

    got_fwd, got_bwd = swap(
        [
            row_terms(back2_fwd, tiles_fwd).astype(jnp.bfloat16),
            row_terms(back2_bwd, tiles_bwd).astype(jnp.bfloat16),
        ]
    )
    near1_fwd = place_rows(got_fwd, src_placer)
    near1_bwd = place_rows(got_bwd, src_placer)
    back1_fwd = (group_of(1) + near_transpose(back2_fwd, dense_fwd) + near1_fwd).astype(
        jnp.bfloat16
    )
    back1_bwd = (group_of(3) + near_transpose(back2_bwd, dense_bwd) + near1_bwd).astype(
        jnp.bfloat16
    )
    (combined,) = swap(
        [(row_terms(back1_fwd, tiles_fwd) + row_terms(back1_bwd, tiles_bwd)).astype(jnp.bfloat16)]
    )
    far_total = place_rows(combined, src_placer)
    skip_back = jnp.einsum("sc,wsn->wcn", w_skip, cot_skip, preferred_element_type=jnp.float32)
    direct = (
        grad_parts[:, :, :channel_count]
        .at[:, output_steps - 1]
        .add(skip_back)
        .reshape(row_count, local_nodes)
    )
    summed = (
        direct
        + near_transpose(back1_fwd, dense_fwd)
        + near_transpose(back1_bwd, dense_bwd)
        + far_total
    )
    grad_hidden = summed.astype(jnp.bfloat16).reshape(shape4).astype(jnp.float32)
    grad_pre = jnp.concatenate(
        [
            grad_hidden * gate_val * (1.0 - filtered * filtered),
            grad_hidden * filtered * gate_val * (1.0 - gate_val),
        ],
        axis=2,
    ).astype(jnp.bfloat16)
    tap_gradients = jnp.einsum(
        "oc,wton->wtcn", w_conv, grad_pre, preferred_element_type=jnp.float32
    )
    input_gradient = jnp.zeros((windows, input_steps, channel_count, local_nodes), jnp.float32)
    input_gradient = input_gradient.at[:, :output_steps].add(tap_gradients[:, :, :channel_count])
    input_gradient = input_gradient.at[:, DILATION_GAP:].add(
        tap_gradients[:, :, channel_count:] + residual_cotangent.astype(jnp.float32)
    )
    grad_wconv = jnp.einsum(
        "wton,wtcn->oc", grad_pre, paired_taps, preferred_element_type=jnp.float32
    )
    grad_bconv = jnp.sum(grad_pre.astype(jnp.float32), axis=(0, 1, 3))
    totals = exchange_sum((grad_wconv, grad_bconv, grad_mix, grad_bmix, grad_skip, grad_bskip))
    grad_count = (
        windows * lax.axis_size("batch") * local_nodes * lax.axis_size("node") * output_steps
    )
    grad_scale = 1.0 / math.sqrt(float(grad_count))
    return (
        residual_stream,
        skip_sum,
        input_gradient.astype(jnp.bfloat16),
        totals[0] * grad_scale,
        totals[1] * grad_scale,
        totals[2] * grad_scale,
        totals[3] * grad_scale,
        totals[4] * grad_scale,
        totals[5] * grad_scale,
    )


def solution(mesh):
    return jax.shard_map(
        shards,
        mesh=mesh,
        in_specs=(
            P("batch", None, None, "node"),
            P(),
            P(),
            P(),
            P(),
            P(),
            P(),
            P("node", None),
            P("node", None),
            P("node", None, None),
            P("node", None, None),
            P("node"),
            P("node"),
            P("batch", None, None, "node"),
            P("batch", None, "node"),
        ),
        out_specs=(
            P("batch", None, None, "node"),
            P("batch", None, "node"),
            P("batch", None, None, "node"),
            P(),
            P(),
            P(),
            P(),
            P(),
            P(),
        ),
        check_vma=False,
    )
```

```python
import math

import jax
import jax.numpy as jnp
from jax import lax
from jax.sharding import PartitionSpec as P

DILATION_GAP = 2


def dense_band(weights, blocks, tile_width):
    shaped = weights.reshape(blocks, tile_width, 1, 3, tile_width)
    row_ids = lax.broadcasted_iota(jnp.int32, (blocks, 1, blocks, 3, 1), 0)
    col_ids = lax.broadcasted_iota(jnp.int32, (blocks, 1, blocks, 3, 1), 2)
    offsets = lax.broadcasted_iota(jnp.int32, (blocks, 1, blocks, 3, 1), 3)
    hits = (col_ids == row_ids + offsets - 1).astype(weights.dtype)
    placed = (shaped * hits).sum(axis=3, dtype=jnp.float32).astype(weights.dtype)
    return placed.reshape(blocks * tile_width, blocks * tile_width)


def spread_onehot(chooser, tile_vals):
    slots, blocks = chooser.shape
    tile_width = tile_vals.shape[2]
    placed = tile_vals[:, :, None, :] * chooser[:, None, :, None]
    return placed.reshape(slots, tile_vals.shape[1], blocks * tile_width)


def near_apply(values, dense):
    return jnp.einsum("mn,kn->mk", values, dense, preferred_element_type=jnp.float32)


def near_transpose(gradient, dense):
    return jnp.einsum("mk,kn->mn", gradient, dense, preferred_element_type=jnp.float32)


def place_rows(pieces, chooser):
    slots, rows, tile_width = pieces.shape
    weighted = pieces.astype(jnp.float32)[:, :, None, :] * chooser.astype(jnp.float32)[
        :, None, :, None
    ]
    return weighted.sum(axis=0).reshape(rows, chooser.shape[1] * tile_width)


def pick_rows(values, chooser):
    rows = values.shape[0]
    blocks = chooser.shape[1]
    shaped = values.reshape(rows, blocks, values.shape[1] // blocks).astype(jnp.float32)
    weighted = shaped[None] * chooser.astype(jnp.float32)[:, None, :, None]
    return weighted.sum(axis=2).astype(jnp.bfloat16)


def exchange_sum(pieces):
    sizes = [piece.size for piece in pieces]
    flat = jnp.concatenate([piece.reshape(-1) for piece in pieces])
    node_count = lax.axis_size("node")
    batch_count = lax.axis_size("batch")
    total = flat.shape[0]
    padded = -(-total // node_count) * node_count
    flat = jnp.pad(flat, (0, padded - total))
    part = lax.all_to_all(
        flat.reshape(node_count, padded // node_count), "node", 0, 0, tiled=True
    ).sum(axis=0)
    part = jnp.broadcast_to(part[None], (batch_count, padded // node_count))
    part = lax.all_to_all(part, "batch", 0, 0, tiled=True).sum(axis=0)
    spread = jnp.broadcast_to(part[None], (node_count, padded // node_count))
    spread = lax.all_to_all(spread, "node", 0, 0, tiled=True).reshape(padded)
    results = []
    offset = 0
    for piece, size in zip(pieces, sizes):
        results.append(spread[offset : offset + size].reshape(piece.shape))
        offset += size
    return tuple(results)


def shards(
    inputs,
    w_conv,
    b_conv,
    w_mix,
    b_mix,
    w_skip,
    b_skip,
    local_fwd,
    local_bwd,
    remote_fwd,
    remote_bwd,
    tile_src,
    tile_dst,
    residual_cotangent,
    cot_skip,
):
    windows, input_steps, channel_count, local_nodes = inputs.shape
    output_steps = input_steps - DILATION_GAP
    tile_width = remote_fwd.shape[1]
    blocks = local_nodes // tile_width
    block_ids = jnp.arange(blocks, dtype=jnp.int32)
    own_src = (tile_src[:, None] == block_ids[None, :]).astype(jnp.bfloat16)
    own_dst = (tile_dst[:, None] == block_ids[None, :]).astype(jnp.bfloat16)
    row_count = windows * output_steps * channel_count
    shape4 = (windows, output_steps, channel_count, local_nodes)
    paired_taps = jnp.concatenate([inputs[:, :output_steps], inputs[:, DILATION_GAP:]], axis=2)
    pre_act = (
        jnp.einsum("oc,wtcn->wton", w_conv, paired_taps, preferred_element_type=jnp.float32)
        + b_conv[None, None, :, None]
    )
    filtered = jnp.tanh(pre_act[:, :, :channel_count])
    gate_val = jax.nn.sigmoid(pre_act[:, :, channel_count:])
    hidden = (filtered * gate_val).astype(jnp.bfloat16)
    flat_hidden = hidden.reshape(row_count, local_nodes)
    dense_fwd = dense_band(local_fwd, blocks, tile_width)
    dense_bwd = dense_band(local_bwd, blocks, tile_width)
    dst_rows = jnp.zeros((own_dst.shape[0], 8, tile_width), jnp.bfloat16)
    dst_rows = dst_rows.at[:, 0, :blocks].set(own_dst)
    tiles_in = lax.all_to_all(
        jnp.concatenate([remote_fwd, remote_bwd, dst_rows], axis=1),
        "node",
        split_axis=0,
        concat_axis=0,
        tiled=True,
    )
    recv_dst = tiles_in[:, 2 * tile_width, :blocks]
    tiles_fwd, tiles_bwd = tiles_in[:, :tile_width], tiles_in[:, tile_width : 2 * tile_width]

    def swap(pieces):
        got_all = lax.all_to_all(
            jnp.concatenate(pieces, axis=1), "node", split_axis=0, concat_axis=0, tiled=True
        )
        return [got_all[:, k * row_count : (k + 1) * row_count] for k in range(len(pieces))]

    def far_terms(columns, tiles):
        return jnp.einsum(
            "smc,sac->sma", columns, tiles, preferred_element_type=jnp.float32
        ).astype(jnp.bfloat16)

    def row_terms(gradient, tiles):
        wanted = pick_rows(gradient, recv_dst)
        return jnp.einsum("sma,sac->smc", wanted, tiles, preferred_element_type=jnp.float32)

    (columns,) = swap([pick_rows(flat_hidden, own_src)])
    far_fwd = place_rows(far_terms(columns, tiles_fwd), recv_dst)
    far_bwd = place_rows(far_terms(columns, tiles_bwd), recv_dst)
    hop_fwd = (near_apply(flat_hidden, dense_fwd) + far_fwd).astype(jnp.bfloat16)
    hop_bwd = (near_apply(flat_hidden, dense_bwd) + far_bwd).astype(jnp.bfloat16)
    columns_fwd, columns_bwd = swap(
        [pick_rows(hop_fwd, own_src), pick_rows(hop_bwd, own_src)]
    )
    far_fwd = place_rows(far_terms(columns_fwd, tiles_fwd), recv_dst)
    far_bwd = place_rows(far_terms(columns_bwd, tiles_bwd), recv_dst)
    two_fwd = (near_apply(hop_fwd, dense_fwd) + far_fwd).astype(jnp.bfloat16)
    two_bwd = (near_apply(hop_bwd, dense_bwd) + far_bwd).astype(jnp.bfloat16)
    stacked_parts = jnp.concatenate(
        [
            hidden,
            hop_fwd.reshape(shape4),
            two_fwd.reshape(shape4),
            hop_bwd.reshape(shape4),
            two_bwd.reshape(shape4),
        ],
        axis=2,
    )
    mixed_features = (
        jnp.einsum("oc,wtcn->wton", w_mix, stacked_parts, preferred_element_type=jnp.float32)
        + b_mix[None, None, :, None]
    )
    residual_stream = (inputs[:, DILATION_GAP:].astype(jnp.float32) + mixed_features).astype(
        jnp.bfloat16
    )
    last_step = hidden[:, output_steps - 1]
    skip_sum = (
        jnp.einsum("sc,wcn->wsn", w_skip, last_step, preferred_element_type=jnp.float32)
        + b_skip[None, :, None]
    ).astype(jnp.bfloat16)
    grad_parts = jnp.einsum(
        "co,wtcn->wton", w_mix, residual_cotangent, preferred_element_type=jnp.float32
    )
    grad_mix = jnp.einsum(
        "wtcn,wton->co", residual_cotangent, stacked_parts, preferred_element_type=jnp.float32
    )
    grad_bmix = jnp.sum(residual_cotangent.astype(jnp.float32), axis=(0, 1, 3))
    grad_skip = jnp.einsum("wsn,wcn->sc", cot_skip, last_step, preferred_element_type=jnp.float32)
    grad_bskip = jnp.sum(cot_skip.astype(jnp.float32), axis=(0, 2))

    def group_of(index):
        return grad_parts[:, :, index * channel_count : (index + 1) * channel_count].reshape(
            row_count, local_nodes
        )

    back2_fwd = group_of(2).astype(jnp.bfloat16)
    back2_bwd = group_of(4).astype(jnp.bfloat16)

    got_fwd, got_bwd = swap(
        [
            row_terms(back2_fwd, tiles_fwd).astype(jnp.bfloat16),
            row_terms(back2_bwd, tiles_bwd).astype(jnp.bfloat16),
        ]
    )
    near1_fwd = place_rows(got_fwd, own_src)
    near1_bwd = place_rows(got_bwd, own_src)
    back1_fwd = (group_of(1) + near_transpose(back2_fwd, dense_fwd) + near1_fwd).astype(
        jnp.bfloat16
    )
    back1_bwd = (group_of(3) + near_transpose(back2_bwd, dense_bwd) + near1_bwd).astype(
        jnp.bfloat16
    )
    (combined,) = swap(
        [(row_terms(back1_fwd, tiles_fwd) + row_terms(back1_bwd, tiles_bwd)).astype(jnp.bfloat16)]
    )
    far_total = place_rows(combined, own_src)
    skip_back = jnp.einsum("sc,wsn->wcn", w_skip, cot_skip, preferred_element_type=jnp.float32)
    direct = (
        grad_parts[:, :, :channel_count]
        .at[:, output_steps - 1]
        .add(skip_back)
        .reshape(row_count, local_nodes)
    )
    summed = (
        direct
        + near_transpose(back1_fwd, dense_fwd)
        + near_transpose(back1_bwd, dense_bwd)
        + far_total
    )
    grad_hidden = summed.astype(jnp.bfloat16).reshape(shape4).astype(jnp.float32)
    grad_pre = jnp.concatenate(
        [
            grad_hidden * gate_val * (1.0 - filtered * filtered),
            grad_hidden * filtered * gate_val * (1.0 - gate_val),
        ],
        axis=2,
    ).astype(jnp.bfloat16)
    tap_gradients = jnp.einsum(
        "oc,wton->wtcn", w_conv, grad_pre, preferred_element_type=jnp.float32
    )
    input_gradient = jnp.zeros((windows, input_steps, channel_count, local_nodes), jnp.float32)
    input_gradient = input_gradient.at[:, :output_steps].add(tap_gradients[:, :, :channel_count])
    input_gradient = input_gradient.at[:, DILATION_GAP:].add(
        tap_gradients[:, :, channel_count:] + residual_cotangent.astype(jnp.float32)
    )
    grad_wconv = jnp.einsum(
        "wton,wtcn->oc", grad_pre, paired_taps, preferred_element_type=jnp.float32
    )
    grad_bconv = jnp.sum(grad_pre.astype(jnp.float32), axis=(0, 1, 3))
    totals = exchange_sum((grad_wconv, grad_bconv, grad_mix, grad_bmix, grad_skip, grad_bskip))
    grad_count = (
        windows * lax.axis_size("batch") * local_nodes * lax.axis_size("node") * output_steps
    )
    grad_scale = 1.0 / math.sqrt(float(grad_count))
    return (
        residual_stream,
        skip_sum,
        input_gradient.astype(jnp.bfloat16),
        totals[0] * grad_scale,
        totals[1] * grad_scale,
        totals[2] * grad_scale,
        totals[3] * grad_scale,
        totals[4] * grad_scale,
        totals[5] * grad_scale,
    )


def solution(mesh):
    return jax.shard_map(
        shards,
        mesh=mesh,
        in_specs=(
            P("batch", None, None, "node"),
            P(),
            P(),
            P(),
            P(),
            P(),
            P(),
            P("node", None),
            P("node", None),
            P("node", None, None),
            P("node", None, None),
            P("node"),
            P("node"),
            P("batch", None, None, "node"),
            P("batch", None, "node"),
        ),
        out_specs=(
            P("batch", None, None, "node"),
            P("batch", None, "node"),
            P("batch", None, None, "node"),
            P(),
            P(),
            P(),
            P(),
            P(),
            P(),
        ),
        check_vma=False,
    )
```

```python
import math

import jax
import jax.numpy as jnp
from jax import lax
from jax.sharding import PartitionSpec as P

DILATION_GAP = 2


def dense_band(weights, blocks, tile_width):
    shaped = weights.reshape(blocks, tile_width, 1, 3, tile_width)
    row_ids = lax.broadcasted_iota(jnp.int32, (blocks, 1, blocks, 3, 1), 0)
    col_ids = lax.broadcasted_iota(jnp.int32, (blocks, 1, blocks, 3, 1), 2)
    offsets = lax.broadcasted_iota(jnp.int32, (blocks, 1, blocks, 3, 1), 3)
    hits = (col_ids == row_ids + offsets - 1).astype(weights.dtype)
    placed = (shaped * hits).sum(axis=3, dtype=jnp.float32).astype(weights.dtype)
    return placed.reshape(blocks * tile_width, blocks * tile_width)


def spread_onehot(chooser, tile_vals):
    slots, blocks = chooser.shape
    tile_width = tile_vals.shape[2]
    placed = tile_vals[:, :, None, :] * chooser[:, None, :, None]
    return placed.reshape(slots, tile_vals.shape[1], blocks * tile_width)


def near_apply(values, dense):
    return jnp.einsum("mn,kn->mk", values, dense, preferred_element_type=jnp.float32)


def near_transpose(gradient, dense):
    return jnp.einsum("mk,kn->mn", gradient, dense, preferred_element_type=jnp.float32)


def place_rows(pieces, placer):
    return jnp.einsum("sma,san->mn", pieces, placer, preferred_element_type=jnp.float32)


def pick_rows(values, placer):
    return jnp.einsum(
        "mn,san->sma", values, placer, preferred_element_type=jnp.float32
    ).astype(jnp.bfloat16)


def exchange_sum(pieces):
    sizes = [piece.size for piece in pieces]
    flat = jnp.concatenate([piece.reshape(-1) for piece in pieces])
    node_count = lax.axis_size("node")
    batch_count = lax.axis_size("batch")
    total = flat.shape[0]
    padded = -(-total // node_count) * node_count
    flat = jnp.pad(flat, (0, padded - total))
    part = lax.all_to_all(
        flat.reshape(node_count, padded // node_count), "node", 0, 0, tiled=True
    ).sum(axis=0)
    part = jnp.broadcast_to(part[None], (batch_count, padded // node_count))
    part = lax.all_to_all(part, "batch", 0, 0, tiled=True).sum(axis=0)
    spread = jnp.broadcast_to(part[None], (node_count, padded // node_count))
    spread = lax.all_to_all(spread, "node", 0, 0, tiled=True).reshape(padded)
    results = []
    offset = 0
    for piece, size in zip(pieces, sizes):
        results.append(spread[offset : offset + size].reshape(piece.shape))
        offset += size
    return tuple(results)


def shards(
    inputs,
    w_conv,
    b_conv,
    w_mix,
    b_mix,
    w_skip,
    b_skip,
    local_fwd,
    local_bwd,
    remote_fwd,
    remote_bwd,
    tile_src,
    tile_dst,
    residual_cotangent,
    cot_skip,
):
    windows, input_steps, channel_count, local_nodes = inputs.shape
    output_steps = input_steps - DILATION_GAP
    tile_width = remote_fwd.shape[1]
    blocks = local_nodes // tile_width
    block_ids = jnp.arange(blocks, dtype=jnp.int32)
    own_src = (tile_src[:, None] == block_ids[None, :]).astype(jnp.bfloat16)
    own_dst = (tile_dst[:, None] == block_ids[None, :]).astype(jnp.bfloat16)
    row_count = windows * output_steps * channel_count
    shape4 = (windows, output_steps, channel_count, local_nodes)
    paired_taps = jnp.concatenate([inputs[:, :output_steps], inputs[:, DILATION_GAP:]], axis=2)
    pre_act = (
        jnp.einsum("oc,wtcn->wton", w_conv, paired_taps, preferred_element_type=jnp.float32)
        + b_conv[None, None, :, None]
    )
    filtered = jnp.tanh(pre_act[:, :, :channel_count])
    gate_val = jax.nn.sigmoid(pre_act[:, :, channel_count:])
    hidden = (filtered * gate_val).astype(jnp.bfloat16)
    flat_hidden = hidden.reshape(row_count, local_nodes)
    eye_tile = jnp.eye(tile_width, dtype=jnp.bfloat16)
    eye_slots = jnp.broadcast_to(eye_tile, (own_src.shape[0], tile_width, tile_width))
    dense_fwd = dense_band(local_fwd, blocks, tile_width)
    dense_bwd = dense_band(local_bwd, blocks, tile_width)
    src_placer = spread_onehot(own_src, eye_slots)
    dst_rows = jnp.zeros((own_dst.shape[0], 8, tile_width), jnp.bfloat16)
    dst_rows = dst_rows.at[:, 0, :blocks].set(own_dst)
    tiles_in = lax.all_to_all(
        jnp.concatenate(
            [remote_fwd, remote_bwd, dst_rows, pick_rows(flat_hidden, src_placer)], axis=1
        ),
        "node",
        split_axis=0,
        concat_axis=0,
        tiled=True,
    )
    columns = tiles_in[:, 2 * tile_width + 8 :]
    recv_dst = tiles_in[:, 2 * tile_width, :blocks]
    dst_placer = spread_onehot(recv_dst, eye_slots)
    tiles_fwd, tiles_bwd = tiles_in[:, :tile_width], tiles_in[:, tile_width : 2 * tile_width]

    def swap(pieces):
        got_all = lax.all_to_all(
            jnp.concatenate(pieces, axis=1), "node", split_axis=0, concat_axis=0, tiled=True
        )
        return [got_all[:, k * row_count : (k + 1) * row_count] for k in range(len(pieces))]

    def far_terms(columns, tiles):
        return jnp.einsum(
            "smc,sac->sma", columns, tiles, preferred_element_type=jnp.float32
        ).astype(jnp.bfloat16)

    def row_terms(gradient, tiles):
        wanted = pick_rows(gradient, dst_placer)
        return jnp.einsum("sma,sac->smc", wanted, tiles, preferred_element_type=jnp.float32)

    far_fwd = place_rows(far_terms(columns, tiles_fwd), dst_placer)
    far_bwd = place_rows(far_terms(columns, tiles_bwd), dst_placer)
    hop_fwd = (near_apply(flat_hidden, dense_fwd) + far_fwd).astype(jnp.bfloat16)
    hop_bwd = (near_apply(flat_hidden, dense_bwd) + far_bwd).astype(jnp.bfloat16)
    columns_fwd, columns_bwd = swap(
        [pick_rows(hop_fwd, src_placer), pick_rows(hop_bwd, src_placer)]
    )
    far_fwd = place_rows(far_terms(columns_fwd, tiles_fwd), dst_placer)
    far_bwd = place_rows(far_terms(columns_bwd, tiles_bwd), dst_placer)
    two_fwd = (near_apply(hop_fwd, dense_fwd) + far_fwd).astype(jnp.bfloat16)
    two_bwd = (near_apply(hop_bwd, dense_bwd) + far_bwd).astype(jnp.bfloat16)
    stacked_parts = jnp.concatenate(
        [
            hidden,
            hop_fwd.reshape(shape4),
            two_fwd.reshape(shape4),
            hop_bwd.reshape(shape4),
            two_bwd.reshape(shape4),
        ],
        axis=2,
    )
    mixed_features = (
        jnp.einsum("oc,wtcn->wton", w_mix, stacked_parts, preferred_element_type=jnp.float32)
        + b_mix[None, None, :, None]
    )
    residual_stream = (inputs[:, DILATION_GAP:].astype(jnp.float32) + mixed_features).astype(
        jnp.bfloat16
    )
    last_step = hidden[:, output_steps - 1]
    skip_sum = (
        jnp.einsum("sc,wcn->wsn", w_skip, last_step, preferred_element_type=jnp.float32)
        + b_skip[None, :, None]
    ).astype(jnp.bfloat16)
    grad_parts = jnp.einsum(
        "co,wtcn->wton", w_mix, residual_cotangent, preferred_element_type=jnp.float32
    )
    grad_mix = jnp.einsum(
        "wtcn,wton->co", residual_cotangent, stacked_parts, preferred_element_type=jnp.float32
    )
    grad_bmix = jnp.sum(residual_cotangent.astype(jnp.float32), axis=(0, 1, 3))
    grad_skip = jnp.einsum("wsn,wcn->sc", cot_skip, last_step, preferred_element_type=jnp.float32)
    grad_bskip = jnp.sum(cot_skip.astype(jnp.float32), axis=(0, 2))

    def group_of(index):
        return grad_parts[:, :, index * channel_count : (index + 1) * channel_count].reshape(
            row_count, local_nodes
        )

    back2_fwd = group_of(2).astype(jnp.bfloat16)
    back2_bwd = group_of(4).astype(jnp.bfloat16)

    got_fwd, got_bwd = swap(
        [
            row_terms(back2_fwd, tiles_fwd).astype(jnp.bfloat16),
            row_terms(back2_bwd, tiles_bwd).astype(jnp.bfloat16),
        ]
    )
    near1_fwd = place_rows(got_fwd, src_placer)
    near1_bwd = place_rows(got_bwd, src_placer)
    back1_fwd = (group_of(1) + near_transpose(back2_fwd, dense_fwd) + near1_fwd).astype(
        jnp.bfloat16
    )
    back1_bwd = (group_of(3) + near_transpose(back2_bwd, dense_bwd) + near1_bwd).astype(
        jnp.bfloat16
    )
    (combined,) = swap(
        [(row_terms(back1_fwd, tiles_fwd) + row_terms(back1_bwd, tiles_bwd)).astype(jnp.bfloat16)]
    )
    far_total = place_rows(combined, src_placer)
    skip_back = jnp.einsum("sc,wsn->wcn", w_skip, cot_skip, preferred_element_type=jnp.float32)
    direct = (
        grad_parts[:, :, :channel_count]
        .at[:, output_steps - 1]
        .add(skip_back)
        .reshape(row_count, local_nodes)
    )
    summed = (
        direct
        + near_transpose(back1_fwd, dense_fwd)
        + near_transpose(back1_bwd, dense_bwd)
        + far_total
    )
    grad_hidden = summed.astype(jnp.bfloat16).reshape(shape4).astype(jnp.float32)
    grad_pre = jnp.concatenate(
        [
            grad_hidden * gate_val * (1.0 - filtered * filtered),
            grad_hidden * filtered * gate_val * (1.0 - gate_val),
        ],
        axis=2,
    ).astype(jnp.bfloat16)
    tap_gradients = jnp.einsum(
        "oc,wton->wtcn", w_conv, grad_pre, preferred_element_type=jnp.float32
    )
    input_gradient = jnp.zeros((windows, input_steps, channel_count, local_nodes), jnp.float32)
    input_gradient = input_gradient.at[:, :output_steps].add(tap_gradients[:, :, :channel_count])
    input_gradient = input_gradient.at[:, DILATION_GAP:].add(
        tap_gradients[:, :, channel_count:] + residual_cotangent.astype(jnp.float32)
    )
    grad_wconv = jnp.einsum(
        "wton,wtcn->oc", grad_pre, paired_taps, preferred_element_type=jnp.float32
    )
    grad_bconv = jnp.sum(grad_pre.astype(jnp.float32), axis=(0, 1, 3))
    totals = exchange_sum((grad_wconv, grad_bconv, grad_mix, grad_bmix, grad_skip, grad_bskip))
    grad_count = (
        windows * lax.axis_size("batch") * local_nodes * lax.axis_size("node") * output_steps
    )
    grad_scale = 1.0 / math.sqrt(float(grad_count))
    return (
        residual_stream,
        skip_sum,
        input_gradient.astype(jnp.bfloat16),
        totals[0] * grad_scale,
        totals[1] * grad_scale,
        totals[2] * grad_scale,
        totals[3] * grad_scale,
        totals[4] * grad_scale,
        totals[5] * grad_scale,
    )


def solution(mesh):
    return jax.shard_map(
        shards,
        mesh=mesh,
        in_specs=(
            P("batch", None, None, "node"),
            P(),
            P(),
            P(),
            P(),
            P(),
            P(),
            P("node", None),
            P("node", None),
            P("node", None, None),
            P("node", None, None),
            P("node"),
            P("node"),
            P("batch", None, None, "node"),
            P("batch", None, "node"),
        ),
        out_specs=(
            P("batch", None, None, "node"),
            P("batch", None, "node"),
            P("batch", None, None, "node"),
            P(),
            P(),
            P(),
            P(),
            P(),
            P(),
        ),
        check_vma=False,
    )
```

```python
import math

import jax
import jax.numpy as jnp
from jax import lax
from jax.sharding import PartitionSpec as P

DILATION_GAP = 2


def dense_band(weights, blocks, tile_width):
    shaped = weights.reshape(blocks, tile_width, 1, 3, tile_width)
    row_ids = lax.broadcasted_iota(jnp.int32, (blocks, 1, blocks, 3, 1), 0)
    col_ids = lax.broadcasted_iota(jnp.int32, (blocks, 1, blocks, 3, 1), 2)
    offsets = lax.broadcasted_iota(jnp.int32, (blocks, 1, blocks, 3, 1), 3)
    hits = (col_ids == row_ids + offsets - 1).astype(weights.dtype)
    placed = (shaped * hits).sum(axis=3, dtype=jnp.float32).astype(weights.dtype)
    return placed.reshape(blocks * tile_width, blocks * tile_width)


def spread_onehot(chooser, tile_vals):
    slots, blocks = chooser.shape
    tile_width = tile_vals.shape[2]
    placed = tile_vals[:, :, None, :] * chooser[:, None, :, None]
    return placed.reshape(slots, tile_vals.shape[1], blocks * tile_width)


def near_apply(values, dense):
    return jnp.einsum("mn,kn->mk", values, dense, preferred_element_type=jnp.float32)


def near_transpose(gradient, dense):
    return jnp.einsum("mk,kn->mn", gradient, dense, preferred_element_type=jnp.float32)


def place_rows(pieces, placer):
    return jnp.einsum("sma,san->mn", pieces, placer, preferred_element_type=jnp.float32)


def pick_rows(values, chooser):
    rows = values.shape[0]
    blocks = chooser.shape[1]
    shaped = values.reshape(rows, blocks, values.shape[1] // blocks).astype(jnp.float32)
    weighted = shaped[None] * chooser.astype(jnp.float32)[:, None, :, None]
    return weighted.sum(axis=2).astype(jnp.bfloat16)


def exchange_sum(pieces):
    sizes = [piece.size for piece in pieces]
    flat = jnp.concatenate([piece.reshape(-1) for piece in pieces])
    node_count = lax.axis_size("node")
    batch_count = lax.axis_size("batch")
    total = flat.shape[0]
    padded = -(-total // node_count) * node_count
    flat = jnp.pad(flat, (0, padded - total))
    part = lax.all_to_all(
        flat.reshape(node_count, padded // node_count), "node", 0, 0, tiled=True
    ).sum(axis=0)
    part = jnp.broadcast_to(part[None], (batch_count, padded // node_count))
    part = lax.all_to_all(part, "batch", 0, 0, tiled=True).sum(axis=0)
    spread = jnp.broadcast_to(part[None], (node_count, padded // node_count))
    spread = lax.all_to_all(spread, "node", 0, 0, tiled=True).reshape(padded)
    results = []
    offset = 0
    for piece, size in zip(pieces, sizes):
        results.append(spread[offset : offset + size].reshape(piece.shape))
        offset += size
    return tuple(results)


def shards(
    inputs,
    w_conv,
    b_conv,
    w_mix,
    b_mix,
    w_skip,
    b_skip,
    local_fwd,
    local_bwd,
    remote_fwd,
    remote_bwd,
    tile_src,
    tile_dst,
    residual_cotangent,
    cot_skip,
):
    windows, input_steps, channel_count, local_nodes = inputs.shape
    output_steps = input_steps - DILATION_GAP
    tile_width = remote_fwd.shape[1]
    blocks = local_nodes // tile_width
    block_ids = jnp.arange(blocks, dtype=jnp.int32)
    own_src = (tile_src[:, None] == block_ids[None, :]).astype(jnp.bfloat16)
    own_dst = (tile_dst[:, None] == block_ids[None, :]).astype(jnp.bfloat16)
    row_count = windows * output_steps * channel_count
    shape4 = (windows, output_steps, channel_count, local_nodes)
    paired_taps = jnp.concatenate([inputs[:, :output_steps], inputs[:, DILATION_GAP:]], axis=2)
    pre_act = (
        jnp.einsum("oc,wtcn->wton", w_conv, paired_taps, preferred_element_type=jnp.float32)
        + b_conv[None, None, :, None]
    )
    filtered = jnp.tanh(pre_act[:, :, :channel_count])
    gate_val = jax.nn.sigmoid(pre_act[:, :, channel_count:])
    hidden = (filtered * gate_val).astype(jnp.bfloat16)
    flat_hidden = hidden.reshape(row_count, local_nodes)
    eye_tile = jnp.eye(tile_width, dtype=jnp.bfloat16)
    eye_slots = jnp.broadcast_to(eye_tile, (own_src.shape[0], tile_width, tile_width))
    dense_fwd = dense_band(local_fwd, blocks, tile_width)
    dense_bwd = dense_band(local_bwd, blocks, tile_width)
    src_placer = spread_onehot(own_src, eye_slots)
    dst_rows = jnp.zeros((own_dst.shape[0], 8, tile_width), jnp.bfloat16)
    dst_rows = dst_rows.at[:, 0, :blocks].set(own_dst)
    tiles_in = lax.all_to_all(
        jnp.concatenate([remote_fwd, remote_bwd, dst_rows], axis=1),
        "node",
        split_axis=0,
        concat_axis=0,
        tiled=True,
    )
    recv_dst = tiles_in[:, 2 * tile_width, :blocks]
    dst_placer = spread_onehot(recv_dst, eye_slots)
    tiles_fwd, tiles_bwd = tiles_in[:, :tile_width], tiles_in[:, tile_width : 2 * tile_width]

    def swap(pieces):
        got_all = lax.all_to_all(
            jnp.concatenate(pieces, axis=1), "node", split_axis=0, concat_axis=0, tiled=True
        )
        return [got_all[:, k * row_count : (k + 1) * row_count] for k in range(len(pieces))]

    def far_terms(columns, tiles):
        return jnp.einsum(
            "smc,sac->sma", columns, tiles, preferred_element_type=jnp.float32
        ).astype(jnp.bfloat16)

    def row_terms(gradient, tiles):
        wanted = pick_rows(gradient, recv_dst)
        return jnp.einsum("sma,sac->smc", wanted, tiles, preferred_element_type=jnp.float32)

    (columns,) = swap([pick_rows(flat_hidden, own_src)])
    far_fwd = place_rows(far_terms(columns, tiles_fwd), dst_placer)
    far_bwd = place_rows(far_terms(columns, tiles_bwd), dst_placer)
    hop_fwd = (near_apply(flat_hidden, dense_fwd) + far_fwd).astype(jnp.bfloat16)
    hop_bwd = (near_apply(flat_hidden, dense_bwd) + far_bwd).astype(jnp.bfloat16)
    columns_fwd, columns_bwd = swap(
        [pick_rows(hop_fwd, own_src), pick_rows(hop_bwd, own_src)]
    )
    far_fwd = place_rows(far_terms(columns_fwd, tiles_fwd), dst_placer)
    far_bwd = place_rows(far_terms(columns_bwd, tiles_bwd), dst_placer)
    two_fwd = (near_apply(hop_fwd, dense_fwd) + far_fwd).astype(jnp.bfloat16)
    two_bwd = (near_apply(hop_bwd, dense_bwd) + far_bwd).astype(jnp.bfloat16)
    stacked_parts = jnp.concatenate(
        [
            hidden,
            hop_fwd.reshape(shape4),
            two_fwd.reshape(shape4),
            hop_bwd.reshape(shape4),
            two_bwd.reshape(shape4),
        ],
        axis=2,
    )
    mixed_features = (
        jnp.einsum("oc,wtcn->wton", w_mix, stacked_parts, preferred_element_type=jnp.float32)
        + b_mix[None, None, :, None]
    )
    residual_stream = (inputs[:, DILATION_GAP:].astype(jnp.float32) + mixed_features).astype(
        jnp.bfloat16
    )
    last_step = hidden[:, output_steps - 1]
    skip_sum = (
        jnp.einsum("sc,wcn->wsn", w_skip, last_step, preferred_element_type=jnp.float32)
        + b_skip[None, :, None]
    ).astype(jnp.bfloat16)
    grad_parts = jnp.einsum(
        "co,wtcn->wton", w_mix, residual_cotangent, preferred_element_type=jnp.float32
    )
    grad_mix = jnp.einsum(
        "wtcn,wton->co", residual_cotangent, stacked_parts, preferred_element_type=jnp.float32
    )
    grad_bmix = jnp.sum(residual_cotangent.astype(jnp.float32), axis=(0, 1, 3))
    grad_skip = jnp.einsum("wsn,wcn->sc", cot_skip, last_step, preferred_element_type=jnp.float32)
    grad_bskip = jnp.sum(cot_skip.astype(jnp.float32), axis=(0, 2))

    def group_of(index):
        return grad_parts[:, :, index * channel_count : (index + 1) * channel_count].reshape(
            row_count, local_nodes
        )

    back2_fwd = group_of(2).astype(jnp.bfloat16)
    back2_bwd = group_of(4).astype(jnp.bfloat16)

    got_fwd, got_bwd = swap(
        [
            row_terms(back2_fwd, tiles_fwd).astype(jnp.bfloat16),
            row_terms(back2_bwd, tiles_bwd).astype(jnp.bfloat16),
        ]
    )
    near1_fwd = place_rows(got_fwd, src_placer)
    near1_bwd = place_rows(got_bwd, src_placer)
    back1_fwd = (group_of(1) + near_transpose(back2_fwd, dense_fwd) + near1_fwd).astype(
        jnp.bfloat16
    )
    back1_bwd = (group_of(3) + near_transpose(back2_bwd, dense_bwd) + near1_bwd).astype(
        jnp.bfloat16
    )
    (combined,) = swap(
        [(row_terms(back1_fwd, tiles_fwd) + row_terms(back1_bwd, tiles_bwd)).astype(jnp.bfloat16)]
    )
    far_total = place_rows(combined, src_placer)
    skip_back = jnp.einsum("sc,wsn->wcn", w_skip, cot_skip, preferred_element_type=jnp.float32)
    direct = (
        grad_parts[:, :, :channel_count]
        .at[:, output_steps - 1]
        .add(skip_back)
        .reshape(row_count, local_nodes)
    )
    summed = (
        direct
        + near_transpose(back1_fwd, dense_fwd)
        + near_transpose(back1_bwd, dense_bwd)
        + far_total
    )
    grad_hidden = summed.astype(jnp.bfloat16).reshape(shape4).astype(jnp.float32)
    grad_pre = jnp.concatenate(
        [
            grad_hidden * gate_val * (1.0 - filtered * filtered),
            grad_hidden * filtered * gate_val * (1.0 - gate_val),
        ],
        axis=2,
    ).astype(jnp.bfloat16)
    tap_gradients = jnp.einsum(
        "oc,wton->wtcn", w_conv, grad_pre, preferred_element_type=jnp.float32
    )
    input_gradient = jnp.zeros((windows, input_steps, channel_count, local_nodes), jnp.float32)
    input_gradient = input_gradient.at[:, :output_steps].add(tap_gradients[:, :, :channel_count])
    input_gradient = input_gradient.at[:, DILATION_GAP:].add(
        tap_gradients[:, :, channel_count:] + residual_cotangent.astype(jnp.float32)
    )
    grad_wconv = jnp.einsum(
        "wton,wtcn->oc", grad_pre, paired_taps, preferred_element_type=jnp.float32
    )
    grad_bconv = jnp.sum(grad_pre.astype(jnp.float32), axis=(0, 1, 3))
    totals = exchange_sum((grad_wconv, grad_bconv, grad_mix, grad_bmix, grad_skip, grad_bskip))
    grad_count = (
        windows * lax.axis_size("batch") * local_nodes * lax.axis_size("node") * output_steps
    )
    grad_scale = 1.0 / math.sqrt(float(grad_count))
    return (
        residual_stream,
        skip_sum,
        input_gradient.astype(jnp.bfloat16),
        totals[0] * grad_scale,
        totals[1] * grad_scale,
        totals[2] * grad_scale,
        totals[3] * grad_scale,
        totals[4] * grad_scale,
        totals[5] * grad_scale,
    )


def solution(mesh):
    return jax.shard_map(
        shards,
        mesh=mesh,
        in_specs=(
            P("batch", None, None, "node"),
            P(),
            P(),
            P(),
            P(),
            P(),
            P(),
            P("node", None),
            P("node", None),
            P("node", None, None),
            P("node", None, None),
            P("node"),
            P("node"),
            P("batch", None, None, "node"),
            P("batch", None, "node"),
        ),
        out_specs=(
            P("batch", None, None, "node"),
            P("batch", None, "node"),
            P("batch", None, None, "node"),
            P(),
            P(),
            P(),
            P(),
            P(),
            P(),
        ),
        check_vma=False,
    )
```

```python
import math

import jax
import jax.numpy as jnp
from jax import lax
from jax.sharding import PartitionSpec as P

DILATION_GAP = 2


def dense_band(weights, blocks, tile_width):
    shaped = weights.reshape(blocks, tile_width, 1, 3, tile_width)
    row_ids = lax.broadcasted_iota(jnp.int32, (blocks, 1, blocks, 3, 1), 0)
    col_ids = lax.broadcasted_iota(jnp.int32, (blocks, 1, blocks, 3, 1), 2)
    offsets = lax.broadcasted_iota(jnp.int32, (blocks, 1, blocks, 3, 1), 3)
    hits = (col_ids == row_ids + offsets - 1).astype(weights.dtype)
    placed = (shaped * hits).sum(axis=3, dtype=jnp.float32).astype(weights.dtype)
    return placed.reshape(blocks * tile_width, blocks * tile_width)


def spread_onehot(chooser, tile_vals):
    slots, blocks = chooser.shape
    tile_width = tile_vals.shape[2]
    placed = tile_vals[:, :, None, :] * chooser[:, None, :, None]
    return placed.reshape(slots, tile_vals.shape[1], blocks * tile_width)


def near_apply(values, dense):
    return jnp.einsum("mn,kn->mk", values, dense, preferred_element_type=jnp.float32)


def near_transpose(gradient, dense):
    return jnp.einsum("mk,kn->mn", gradient, dense, preferred_element_type=jnp.float32)


def place_rows(pieces, placer):
    return jnp.einsum("sma,san->mn", pieces, placer, preferred_element_type=jnp.float32)


def pick_rows(values, placer):
    return jnp.einsum(
        "mn,san->sma", values, placer, preferred_element_type=jnp.float32
    ).astype(jnp.bfloat16)


def exchange_sum(pieces, rider):
    sizes = [piece.size for piece in pieces]
    flat = jnp.concatenate([piece.reshape(-1) for piece in pieces])
    node_count = lax.axis_size("node")
    batch_count = lax.axis_size("batch")
    total = flat.shape[0]
    padded = -(-total // node_count) * node_count
    flat = jnp.pad(flat, (0, padded - total))
    part = lax.all_to_all(
        flat.reshape(node_count, padded // node_count), "node", 0, 0, tiled=True
    ).sum(axis=0)
    part, rider = lax.optimization_barrier((part, rider))
    part = jnp.broadcast_to(part[None], (batch_count, padded // node_count))
    part = lax.all_to_all(part, "batch", 0, 0, tiled=True).sum(axis=0)
    spread = jnp.broadcast_to(part[None], (node_count, padded // node_count))
    spread = lax.all_to_all(spread, "node", 0, 0, tiled=True).reshape(padded)
    results = []
    offset = 0
    for piece, size in zip(pieces, sizes):
        results.append(spread[offset : offset + size].reshape(piece.shape))
        offset += size
    return tuple(results), rider


def shards(
    inputs,
    w_conv,
    b_conv,
    w_mix,
    b_mix,
    w_skip,
    b_skip,
    local_fwd,
    local_bwd,
    remote_fwd,
    remote_bwd,
    tile_src,
    tile_dst,
    residual_cotangent,
    cot_skip,
):
    windows, input_steps, channel_count, local_nodes = inputs.shape
    output_steps = input_steps - DILATION_GAP
    tile_width = remote_fwd.shape[1]
    blocks = local_nodes // tile_width
    block_ids = jnp.arange(blocks, dtype=jnp.int32)
    own_src = (tile_src[:, None] == block_ids[None, :]).astype(jnp.bfloat16)
    own_dst = (tile_dst[:, None] == block_ids[None, :]).astype(jnp.bfloat16)
    row_count = windows * output_steps * channel_count
    shape4 = (windows, output_steps, channel_count, local_nodes)
    paired_taps = jnp.concatenate([inputs[:, :output_steps], inputs[:, DILATION_GAP:]], axis=2)
    pre_act = (
        jnp.einsum("oc,wtcn->wton", w_conv, paired_taps, preferred_element_type=jnp.float32)
        + b_conv[None, None, :, None]
    )
    filtered = jnp.tanh(pre_act[:, :, :channel_count])
    gate_val = jax.nn.sigmoid(pre_act[:, :, channel_count:])
    hidden = (filtered * gate_val).astype(jnp.bfloat16)
    flat_hidden = hidden.reshape(row_count, local_nodes)
    eye_tile = jnp.eye(tile_width, dtype=jnp.bfloat16)
    eye_slots = jnp.broadcast_to(eye_tile, (own_src.shape[0], tile_width, tile_width))
    dense_fwd = dense_band(local_fwd, blocks, tile_width)
    dense_bwd = dense_band(local_bwd, blocks, tile_width)
    src_placer = spread_onehot(own_src, eye_slots)
    dst_rows = jnp.zeros((own_dst.shape[0], 8, tile_width), jnp.bfloat16)
    dst_rows = dst_rows.at[:, 0, :blocks].set(own_dst)
    tiles_in = lax.all_to_all(
        jnp.concatenate([remote_fwd, remote_bwd, dst_rows], axis=1),
        "node",
        split_axis=0,
        concat_axis=0,
        tiled=True,
    )
    recv_dst = tiles_in[:, 2 * tile_width, :blocks]
    dst_placer = spread_onehot(recv_dst, eye_slots)
    tiles_fwd, tiles_bwd = tiles_in[:, :tile_width], tiles_in[:, tile_width : 2 * tile_width]

    def swap(pieces):
        got_all = lax.all_to_all(
            jnp.concatenate(pieces, axis=1), "node", split_axis=0, concat_axis=0, tiled=True
        )
        return [got_all[:, k * row_count : (k + 1) * row_count] for k in range(len(pieces))]

    def far_terms(columns, tiles):
        return jnp.einsum(
            "smc,sac->sma", columns, tiles, preferred_element_type=jnp.float32
        ).astype(jnp.bfloat16)

    def row_terms(gradient, tiles):
        wanted = pick_rows(gradient, dst_placer)
        return jnp.einsum("sma,sac->smc", wanted, tiles, preferred_element_type=jnp.float32)

    (columns,) = swap([pick_rows(flat_hidden, src_placer)])
    far_fwd = place_rows(far_terms(columns, tiles_fwd), dst_placer)
    far_bwd = place_rows(far_terms(columns, tiles_bwd), dst_placer)
    hop_fwd = (near_apply(flat_hidden, dense_fwd) + far_fwd).astype(jnp.bfloat16)
    hop_bwd = (near_apply(flat_hidden, dense_bwd) + far_bwd).astype(jnp.bfloat16)
    columns_fwd, columns_bwd = swap(
        [pick_rows(hop_fwd, src_placer), pick_rows(hop_bwd, src_placer)]
    )
    far_fwd = place_rows(far_terms(columns_fwd, tiles_fwd), dst_placer)
    far_bwd = place_rows(far_terms(columns_bwd, tiles_bwd), dst_placer)
    two_fwd = (near_apply(hop_fwd, dense_fwd) + far_fwd).astype(jnp.bfloat16)
    two_bwd = (near_apply(hop_bwd, dense_bwd) + far_bwd).astype(jnp.bfloat16)
    stacked_parts = jnp.concatenate(
        [
            hidden,
            hop_fwd.reshape(shape4),
            two_fwd.reshape(shape4),
            hop_bwd.reshape(shape4),
            two_bwd.reshape(shape4),
        ],
        axis=2,
    )
    mixed_features = (
        jnp.einsum("oc,wtcn->wton", w_mix, stacked_parts, preferred_element_type=jnp.float32)
        + b_mix[None, None, :, None]
    )
    residual_stream = (inputs[:, DILATION_GAP:].astype(jnp.float32) + mixed_features).astype(
        jnp.bfloat16
    )
    last_step = hidden[:, output_steps - 1]
    skip_sum = (
        jnp.einsum("sc,wcn->wsn", w_skip, last_step, preferred_element_type=jnp.float32)
        + b_skip[None, :, None]
    ).astype(jnp.bfloat16)
    grad_parts = jnp.einsum(
        "co,wtcn->wton", w_mix, residual_cotangent, preferred_element_type=jnp.float32
    )
    grad_mix = jnp.einsum(
        "wtcn,wton->co", residual_cotangent, stacked_parts, preferred_element_type=jnp.float32
    )
    grad_bmix = jnp.sum(residual_cotangent.astype(jnp.float32), axis=(0, 1, 3))
    grad_skip = jnp.einsum("wsn,wcn->sc", cot_skip, last_step, preferred_element_type=jnp.float32)
    grad_bskip = jnp.sum(cot_skip.astype(jnp.float32), axis=(0, 2))

    def group_of(index):
        return grad_parts[:, :, index * channel_count : (index + 1) * channel_count].reshape(
            row_count, local_nodes
        )

    back2_fwd = group_of(2).astype(jnp.bfloat16)
    back2_bwd = group_of(4).astype(jnp.bfloat16)

    got_fwd, got_bwd = swap(
        [
            row_terms(back2_fwd, tiles_fwd).astype(jnp.bfloat16),
            row_terms(back2_bwd, tiles_bwd).astype(jnp.bfloat16),
        ]
    )
    near1_fwd = place_rows(got_fwd, src_placer)
    near1_bwd = place_rows(got_bwd, src_placer)
    back1_fwd = (group_of(1) + near_transpose(back2_fwd, dense_fwd) + near1_fwd).astype(
        jnp.bfloat16
    )
    back1_bwd = (group_of(3) + near_transpose(back2_bwd, dense_bwd) + near1_bwd).astype(
        jnp.bfloat16
    )
    (combined,) = swap(
        [(row_terms(back1_fwd, tiles_fwd) + row_terms(back1_bwd, tiles_bwd)).astype(jnp.bfloat16)]
    )
    far_total = place_rows(combined, src_placer)
    skip_back = jnp.einsum("sc,wsn->wcn", w_skip, cot_skip, preferred_element_type=jnp.float32)
    direct = (
        grad_parts[:, :, :channel_count]
        .at[:, output_steps - 1]
        .add(skip_back)
        .reshape(row_count, local_nodes)
    )
    summed = (
        direct
        + near_transpose(back1_fwd, dense_fwd)
        + near_transpose(back1_bwd, dense_bwd)
        + far_total
    )
    grad_hidden = summed.astype(jnp.bfloat16).reshape(shape4).astype(jnp.float32)
    grad_pre = jnp.concatenate(
        [
            grad_hidden * gate_val * (1.0 - filtered * filtered),
            grad_hidden * filtered * gate_val * (1.0 - gate_val),
        ],
        axis=2,
    ).astype(jnp.bfloat16)
    grad_wconv = jnp.einsum(
        "wton,wtcn->oc", grad_pre, paired_taps, preferred_element_type=jnp.float32
    )
    grad_bconv = jnp.sum(grad_pre.astype(jnp.float32), axis=(0, 1, 3))
    totals, late_pre = exchange_sum(
        (grad_wconv, grad_bconv, grad_mix, grad_bmix, grad_skip, grad_bskip), grad_pre
    )
    tap_gradients = jnp.einsum(
        "oc,wton->wtcn", w_conv, late_pre, preferred_element_type=jnp.float32
    )
    input_gradient = jnp.zeros((windows, input_steps, channel_count, local_nodes), jnp.float32)
    input_gradient = input_gradient.at[:, :output_steps].add(tap_gradients[:, :, :channel_count])
    input_gradient = input_gradient.at[:, DILATION_GAP:].add(
        tap_gradients[:, :, channel_count:] + residual_cotangent.astype(jnp.float32)
    )
    grad_count = (
        windows * lax.axis_size("batch") * local_nodes * lax.axis_size("node") * output_steps
    )
    grad_scale = 1.0 / math.sqrt(float(grad_count))
    return (
        residual_stream,
        skip_sum,
        input_gradient.astype(jnp.bfloat16),
        totals[0] * grad_scale,
        totals[1] * grad_scale,
        totals[2] * grad_scale,
        totals[3] * grad_scale,
        totals[4] * grad_scale,
        totals[5] * grad_scale,
    )


def solution(mesh):
    return jax.shard_map(
        shards,
        mesh=mesh,
        in_specs=(
            P("batch", None, None, "node"),
            P(),
            P(),
            P(),
            P(),
            P(),
            P(),
            P("node", None),
            P("node", None),
            P("node", None, None),
            P("node", None, None),
            P("node"),
            P("node"),
            P("batch", None, None, "node"),
            P("batch", None, "node"),
        ),
        out_specs=(
            P("batch", None, None, "node"),
            P("batch", None, "node"),
            P("batch", None, None, "node"),
            P(),
            P(),
            P(),
            P(),
            P(),
            P(),
        ),
        check_vma=False,
    )
```
